256 devices in a mesh: gx: 32 (over z, y), gy: 8 (over x, core).
Axes of the slice: x: 4, y: 4, z: 8, core: 2. Of those that a mesh axis runs over, the one named last changes fastest.
Arguments:
- fields: float32 [4, 8, 4096, 1024], P(None, None, 'gx', 'gy'), may hold values from -6 to 6
- shift_x: float32 [8, 4096, 1024], P(None, 'gx', 'gy'), may hold values from -0.5 to 0.5
- shift_y: float32 [8, 4096, 1024], P(None, 'gx', 'gy'), may hold values from -0.5 to 0.5
- block_offset: int32 [256, 8], P(None, 'gy'), may hold values from -23 to 23, as said below
- group_inverse: float32 [8, 4096, 128], P(None, 'gx'), as said below
- lower_coupling: float32 [8, 32], P(None, 'gx'), as said below
- upper_coupling: float32 [8, 32], P(None, 'gx'), as said below
Outputs:
- wind_fields: float32 [2, 8, 4096, 1024], P(None, None, 'gx', 'gy')
- tracers: float32 [2, 8, 4096, 1024], P(None, None, 'gx', 'gy')
The draws below stay inside these ranges and needn't reach their ends.
Inputs may be any that keep to these rules, and one draw needn't show every extreme that they name: `block_offset`: within each aligned run of 8 x-blocks (the blocks of 128 consecutive columns at one y-block), every block departs from a block in the same run or in one of the two runs before or after it, and that run lies inside the grid; at most 4 blocks of a run depart from any one run, and exactly 4 depart from a run two runs away. `group_inverse`: entries are positive. `lower_coupling`: Negative. `upper_coupling`: Negative.
All inputs are finite; a program needn't handle non-finite values.
Results may differ from the reference program's by a relative error of at most 0.0003.
Values sent between devices are 32-bit elements; how exact they have to be, the bound alone decides.
No kernel may reach another device: no remote copies, remote signals or barrier semaphores. Data moves between devices by JAX's collectives and lax.ppermute only.
A program may use at most 128 MiB of HBM per device.

```python
import math
import jax
import jax.numpy as jnp
from jax import lax

FIELDS = 4
MODEL_LEVELS = 8
CX = 128
CY = 128
BX = 16
NBX = 8
CAP = 4
NX = 4096
NY = 1024
NXB = 256
PADX = 258
N_GX = 32
N_GY = 8


def draw_block_offset(key, part):
    root_random_key = jax.random.fold_in(key, 3)
    score_key = jax.random.fold_in(root_random_key, 1)
    pick_key = jax.random.fold_in(root_random_key, 2)
    local_key = jax.random.fold_in(root_random_key, 3)
    group_place = jnp.arange(N_GX, dtype=jnp.int32)[:, None, None]
    row_place = jnp.arange(N_GY, dtype=jnp.int32)[None, None, :]
    parity_side = jnp.where((group_place + row_place) % 2 == 1, -2, 2)
    primary = jnp.where(group_place < 2, 2, jnp.where(group_place >= N_GX - 2, -2, parity_side))
    inside = jnp.arange(NBX, dtype=jnp.int32)[None, :, None]
    scores = jax.random.randint(score_key, (N_GX, NBX, N_GY), 0, 1 << 20) * NBX + inside
    ranking = jnp.argsort(jnp.argsort(scores, axis=1), axis=1)
    picked = jax.random.randint(pick_key, (N_GX, NBX, N_GY), 0, 4)
    others = picked - 2 + jnp.where(primary == -2, 1, 0)
    others = jnp.clip(others, -group_place, N_GX - 1 - group_place)
    distance = jnp.where(ranking < CAP, primary, others)
    source_random = jax.random.randint(local_key, (N_GX, NBX, N_GY), 0, NBX)
    edge_source = jnp.where(primary == -2, 0, NBX - 1)
    source_local = jnp.where(ranking == 0, edge_source, source_random)
    offsets = inside - source_local - distance * NBX
    return offsets.reshape(NXB, N_GY).astype(jnp.int32)


def interface_draw(key):
    root_random_key = jax.random.fold_in(key, 4)
    coarse_random_key, diagonal_random_key, category_random_key, gentle_random_key, quick_random_key, surge_random_key, level_depth_key = jax.random.split(root_random_key, 7)
    rows_in = (jnp.arange(NX, dtype=jnp.int32) % CX)[:, None]
    cols_in = jnp.arange(CX, dtype=jnp.int32)[None, :]
    spacing = jnp.abs(rows_in - cols_in).astype(jnp.float32)
    smooth = jnp.exp(-spacing / (2.0 * CX))
    rough = jax.random.uniform(coarse_random_key, (MODEL_LEVELS, NX, CX), jnp.float32, -1.0, 1.0)
    diagonal = jax.random.uniform(diagonal_random_key, (MODEL_LEVELS, NX, 1), jnp.float32, 0.3, 0.9)
    on_diagonal = jnp.where(rows_in == cols_in, 1.0, 0.0).astype(jnp.float32)
    entries = smooth[None] * (1.0 + 0.3 * rough) + on_diagonal[None] * diagonal
    rows_float = rows_in.astype(jnp.float32)
    ramp_first = jnp.exp(-3.9 * (CX - 1.0 - rows_float) / (CX - 1.0))
    ramp_last = jnp.exp(-3.9 * rows_float / (CX - 1.0))
    first_column = ramp_first[None] * (1.0 + 0.3 * rough[:, :, 0:1])
    last_column = ramp_last[None] * (1.0 + 0.3 * rough[:, :, CX - 1:CX])
    entries = jnp.where(cols_in[None] == 0, first_column, jnp.where(cols_in[None] == CX - 1, last_column, entries))
    inverse = entries / math.sqrt(CX)
    blocks = inverse.reshape(MODEL_LEVELS, N_GX, CX, CX)
    far_first = blocks[:, :, CX - 1, 0]
    far_last = blocks[:, :, 0, CX - 1]
    level_rank = jax.random.permutation(category_random_key, MODEL_LEVELS)
    slow_count = max(1, MODEL_LEVELS // 2)
    gentle_level = (level_rank < slow_count)[None, :, None]
    slow_rate = min(math.exp(math.log(0.2) / N_GX), 0.95)
    gentle_rate_values = slow_rate * jax.random.uniform(gentle_random_key, (2, MODEL_LEVELS, N_GX), jnp.float32, 0.985, 1.0)
    quick_rate_values = jax.random.uniform(quick_random_key, (2, MODEL_LEVELS, N_GX), jnp.float32, 0.57, 0.6)
    surge_level_draw = jax.random.uniform(surge_random_key, (2, MODEL_LEVELS, N_GX), jnp.float32, 0.0, 1.0)
    surge_level_depth = jax.random.uniform(level_depth_key, (2, MODEL_LEVELS, N_GX), jnp.float32, 0.5, 0.8)
    level_rates = jnp.where(gentle_level, gentle_rate_values, quick_rate_values) * jnp.where(surge_level_draw < 0.1, surge_level_depth, 1.0)
    lower = -level_rates[0] / far_first
    upper = -level_rates[1] / far_last
    return (inverse, lower, upper)


def draw_group_inverse(key, part):
    return interface_draw(key)[0]


def draw_lower_coupling(key, part):
    return interface_draw(key)[1]


def draw_upper_coupling(key, part):
    return interface_draw(key)[2]


def levels(stream_key, dims, shards, low, largest):
    gain = 1.0
    for axis_at, shards_of in shards:
        draws = jax.random.uniform(jax.random.fold_in(jax.random.fold_in(stream_key, 6), axis_at), (shards_of,), jnp.float32, low / len(shards), largest / len(shards))
        gain = gain * jnp.repeat(jnp.exp(draws), dims[axis_at] // shards_of).reshape((-1,) + (1,) * (len(dims) - 1 - axis_at))
    return gain


def scatter_about(key, dims, width, bound, cuts=(), kind=jnp.bfloat16):
    drawn = jax.random.normal(key, dims, jnp.float32) * width
    if len(cuts) > 0:
        drawn = levels(key, dims, cuts, -0.22, 0.18) * drawn
    return jnp.clip(drawn, min=-bound, max=bound).astype(kind)


def setup_inputs(seed: int = 0) -> dict:
    arg_keys = jax.random.split(jax.random.key(seed), 8)
    return {
        "fields": scatter_about(arg_keys[0], (FIELDS, MODEL_LEVELS, NX, NY), 1.0, 6.0, ((2, 32), (3, 8)), jnp.float32),
        "shift_x": jnp.clip(jax.random.uniform(arg_keys[1], (MODEL_LEVELS, NX, NY), jnp.float32, -0.5, 0.5) * levels(arg_keys[1], (MODEL_LEVELS, NX, NY), ((1, 32), (2, 8)), -0.4, 0.0), -0.5, 0.5),
        "shift_y": jnp.clip(jax.random.uniform(arg_keys[2], (MODEL_LEVELS, NX, NY), jnp.float32, -0.5, 0.5) * levels(arg_keys[2], (MODEL_LEVELS, NX, NY), ((1, 32), (2, 8)), -0.4, 0.0), -0.5, 0.5),
        "block_offset": draw_block_offset(jax.random.fold_in(arg_keys[7], 71), 0),
        "group_inverse": draw_group_inverse(jax.random.fold_in(arg_keys[7], 71), 0),
        "lower_coupling": draw_lower_coupling(jax.random.fold_in(arg_keys[7], 71), 0),
        "upper_coupling": draw_upper_coupling(jax.random.fold_in(arg_keys[7], 71), 0),
    }


PRECISE = lax.Precision.HIGHEST

def lagrange(displace):
    position = -displace
    weights = []
    for target in range(-2, 3):
        factor = jnp.ones_like(position)
        for anchor in range(-2, 3):
            if anchor != target:
                factor = factor * ((position - anchor) / (target - anchor))
        weights.append(factor)
    return weights

def interpolate(window, across, along, span_x, span_y):
    weights_x = lagrange(across)
    weights_y = lagrange(along)
    running_total = None
    for column_tap in range(5):
        partial_sum = weights_y[0] * window[..., column_tap:column_tap + span_x, 0:span_y]
        for row_tap in range(1, 5):
            partial_sum = partial_sum + weights_y[row_tap] * window[..., column_tap:column_tap + span_x, row_tap:row_tap + span_y]
        tap_term = weights_x[column_tap] * partial_sum
        running_total = tap_term if running_total is None else running_total + tap_term
    return running_total

def advect(fields, shift_x, shift_y, block_offset):
    padded = jnp.pad(fields, ((0, 0), (0, 0), (PADX, PADX), (2, 2)))
    blocks_x = NX // BX
    blocks_y = N_GY

    def one_block(flat_index):
        column_block = flat_index // blocks_y
        row_block = flat_index % blocks_y
        offset_here = block_offset[column_block, row_block].astype(jnp.int32)
        start_x = ((column_block - offset_here) * BX + PADX - 2).astype(jnp.int32)
        start_y = (row_block * CY).astype(jnp.int32)
        zero_index = jnp.zeros((), jnp.int32)
        window = lax.dynamic_slice(padded, (zero_index, zero_index, start_x, start_y), (FIELDS, MODEL_LEVELS, BX + 4, CY + 4))
        root_x = (column_block * BX).astype(jnp.int32)
        across = lax.dynamic_slice(shift_x, (zero_index, root_x, start_y), (MODEL_LEVELS, BX, CY))
        along = lax.dynamic_slice(shift_y, (zero_index, root_x, start_y), (MODEL_LEVELS, BX, CY))
        return interpolate(window, across[None], along[None], BX, CY)
    gathered = lax.map(one_block, jnp.arange(blocks_x * blocks_y, dtype=jnp.int32))
    gathered = gathered.reshape(blocks_x, blocks_y, FIELDS, MODEL_LEVELS, BX, CY)
    return gathered.transpose(2, 3, 0, 4, 1, 5).reshape(FIELDS, MODEL_LEVELS, NX, NY)

def implicit_sweep(winds_in, group_inverse, lower_coupling, upper_coupling):
    chains = N_GX
    inverse = group_inverse.reshape(MODEL_LEVELS, chains, CX, CX)
    right_side = winds_in.reshape(2, MODEL_LEVELS, chains, CX, NY)
    local_solve = jnp.einsum('ldij,wldjy->wldiy', inverse, right_side, precision=PRECISE)
    first_row = local_solve[:, :, :, 0, :]
    last_row = local_solve[:, :, :, CX - 1, :]
    left_spike = inverse[:, :, :, 0] * lower_coupling[:, :, None]
    right_spike = inverse[:, :, :, CX - 1] * upper_coupling[:, :, None]
    lead_left = left_spike[:, :, 0]
    tail_left = left_spike[:, :, CX - 1]
    lead_right = right_spike[:, :, 0]
    tail_right = right_spike[:, :, CX - 1]
    unknowns = 2 * chains
    matrix = jnp.broadcast_to(jnp.eye(unknowns, dtype=jnp.float32), (MODEL_LEVELS, unknowns, unknowns))
    chain_index = jnp.arange(chains, dtype=jnp.int32)
    later_chain = chain_index[1:]
    early_chain = chain_index[:-1]
    matrix = matrix.at[:, 2 * later_chain, 2 * later_chain - 1].set(lead_left[:, 1:])
    matrix = matrix.at[:, 2 * early_chain, 2 * early_chain + 2].set(lead_right[:, :-1])
    matrix = matrix.at[:, 2 * later_chain + 1, 2 * later_chain - 1].set(tail_left[:, 1:])
    matrix = matrix.at[:, 2 * early_chain + 1, 2 * early_chain + 2].set(tail_right[:, :-1])
    reduced_side = jnp.stack([first_row, last_row], axis=3)
    reduced_side = reduced_side.transpose(1, 2, 3, 0, 4).reshape(MODEL_LEVELS, unknowns, 2 * NY)
    solved = jnp.linalg.solve(matrix, reduced_side).reshape(MODEL_LEVELS, chains, 2, 2, NY)
    first_all = solved[:, :, 0].transpose(2, 0, 1, 3)
    last_all = solved[:, :, 1].transpose(2, 0, 1, 3)
    zero_chain = jnp.zeros_like(first_all[:, :, :1])
    left_value = jnp.concatenate([zero_chain, last_all[:, :, :-1]], axis=2)
    right_value = jnp.concatenate([first_all[:, :, 1:], zero_chain], axis=2)
    wind_fields = local_solve - left_spike[None, :, :, :, None] * left_value[:, :, :, None, :] - right_spike[None, :, :, :, None] * right_value[:, :, :, None, :]
    return wind_fields.reshape(2, MODEL_LEVELS, NX, NY)

def reference(fields, shift_x, shift_y, block_offset, group_inverse, lower_coupling, upper_coupling):
    advected = advect(fields, shift_x, shift_y, block_offset)
    wind_fields = implicit_sweep(advected[0:2], group_inverse, lower_coupling, upper_coupling)
    return (wind_fields, advected[2:4])
```

```python
import jax
import jax.numpy as jnp
from jax import lax
from jax.sharding import PartitionSpec as P

BX = 16


PRECISE = lax.Precision.HIGHEST


def padded_2(block, sides, width):
    for axis, dim in sides:
        count = lax.axis_size(axis)
        forward = [(i, i + 1) for i in range(count - 1)]
        backward = [(target, source) for source, target in forward]
        low = lax.ppermute(
            lax.slice_in_dim(block, block.shape[dim] - width, None, axis=dim), axis, forward
        )
        high = lax.ppermute(lax.slice_in_dim(block, 0, width, axis=dim), axis, backward)
        block = jnp.concatenate([low, block, high], axis=dim)
    return block


def shifted_2(value, axis, steps):
    count = lax.axis_size(axis)
    leading, last = (max(0, -steps), min(count, count - steps))
    return lax.ppermute(value, axis, [(source, source + steps) for source in range(leading, last)])


def lagrange(displace):
    position = -displace
    weights = []
    for target in range(-2, 3):
        factor = jnp.ones_like(position)
        for anchor in range(-2, 3):
            if anchor != target:
                factor = factor * ((position - anchor) / (target - anchor))
        weights.append(factor)
    return weights


def interpolate(window, across, along, span_x, span_y):
    weights_x = lagrange(across)
    weights_y = lagrange(along)
    running_total = None
    for column_tap in range(5):
        partial_sum = weights_y[0] * window[..., column_tap : column_tap + span_x, 0:span_y]
        for row_tap in range(1, 5):
            partial_sum = (
                partial_sum
                + weights_y[row_tap]
                * window[..., column_tap : column_tap + span_x, row_tap : row_tap + span_y]
            )
        tap_term = weights_x[column_tap] * partial_sum
        running_total = tap_term if running_total is None else running_total + tap_term
    return running_total


def interface_solve(packed_all, position, width):
    count = packed_all.shape[0]
    p = None
    q = None
    alphas, betas, lefts_p, lefts_q = [], [], [], []
    for j in range(count):
        first_j = packed_all[j, 0:width]
        last_j = packed_all[j, width : 2 * width]
        coef = packed_all[j, 2 * width]
        lead_left = coef[:, 0:1]
        tail_left = coef[:, 1:2]
        lead_right = coef[:, 2:3]
        tail_right = coef[:, 3:4]
        if p is None:
            pivot = jnp.ones_like(lead_left)
            alpha = first_j
            beta = -lead_right
            p_new = last_j
            q_new = -tail_right
        else:
            pivot = 1.0 + lead_left * q
            alpha = (first_j - lead_left * p) / pivot
            beta = -lead_right / pivot
            p_new = last_j - tail_left * p - tail_left * q * alpha
            q_new = -(tail_left * q * beta) - tail_right
        alphas.append(alpha)
        betas.append(beta)
        lefts_p.append(p)
        lefts_q.append(q)
        p, q = p_new, q_new
    firsts = [None] * count
    ahead = None
    for j in range(count - 1, -1, -1):
        firsts[j] = alphas[j] if ahead is None else alphas[j] + betas[j] * ahead
        ahead = firsts[j]
    zero = jnp.zeros_like(firsts[0])
    left_values = [zero] + [lefts_p[j] + lefts_q[j] * firsts[j] for j in range(1, count)]
    right_values = firsts[1:] + [zero]
    left_value = jnp.stack(left_values)[position]
    right_value = jnp.stack(right_values)[position]
    return left_value, right_value


def local(fields, shift_x, shift_y, block_offset, group_inverse, lower_coupling, upper_coupling):
    field_count, level_count, columns, rows_here = fields.shape
    block_count = columns // BX
    position = lax.axis_index("gx")
    padded = padded_2(fields, (("gx", 2), ("gy", 3)), 2)
    offsets = block_offset[:, 0]
    inside = jnp.arange(block_count, dtype=jnp.int32)
    own_offset = lax.dynamic_slice_in_dim(offsets, position * block_count, block_count)
    shifted = []
    for step_distance in (2, 1, -1, -2):
        shifted.append(shifted_2(padded, "gx", step_distance))
    window_field = jnp.concatenate(
        [
            shifted[0][:, :, 0 : columns + 2],
            shifted[1][:, :, 2 : columns + 2],
            padded[:, :, 2 : columns + 2],
            shifted[2][:, :, 2 : columns + 2],
            shifted[3][:, :, 2 : columns + 4],
        ],
        axis=2,
    )
    starts = (inside - own_offset) * BX + 2 * columns
    windows = jnp.stack(
        [
            lax.dynamic_slice_in_dim(window_field, starts[column_block], BX + 4, 2)
            for column_block in range(block_count)
        ]
    )
    across = shift_x.reshape(level_count, block_count, BX, rows_here).transpose(1, 0, 2, 3)[:, None]
    along = shift_y.reshape(level_count, block_count, BX, rows_here).transpose(1, 0, 2, 3)[:, None]
    interpolated = interpolate(windows, across, along, BX, rows_here)
    advected = interpolated.transpose(1, 2, 0, 3, 4).reshape(
        field_count, level_count, columns, rows_here
    )
    local_solve = jnp.einsum("lij,wljy->wliy", group_inverse, advected[0:2], precision=PRECISE)
    lower_here = lower_coupling[:, 0]
    upper_here = upper_coupling[:, 0]
    left_spike = group_inverse[:, :, 0] * lower_here[:, None]
    right_spike = group_inverse[:, :, columns - 1] * upper_here[:, None]
    coef = jnp.stack(
        [left_spike[:, 0], left_spike[:, columns - 1], right_spike[:, 0], right_spike[:, columns - 1]],
        axis=-1,
    )
    coef_rows = jnp.pad(coef, ((0, 0), (0, rows_here - 4)))
    first_row = local_solve[:, :, 0, :]
    last_row = local_solve[:, :, columns - 1, :]
    packed = jnp.concatenate([first_row, last_row, coef_rows[None]], axis=0)
    packed_all = lax.all_gather(packed, "gx")
    left_value, right_value = interface_solve(packed_all, position, first_row.shape[0])
    wind_fields = (
        local_solve
        - left_spike[None, :, :, None] * left_value[:, :, None, :]
        - right_spike[None, :, :, None] * right_value[:, :, None, :]
    )
    return (wind_fields, advected[2:4])


def solution(mesh):
    return jax.shard_map(
        local,
        mesh=mesh,
        in_specs=(
            P(None, None, "gx", "gy"),
            P(None, "gx", "gy"),
            P(None, "gx", "gy"),
            P(None, "gy"),
            P(None, "gx", None),
            P(None, "gx"),
            P(None, "gx"),
        ),
        out_specs=(P(None, None, "gx", "gy"), P(None, None, "gx", "gy")),
        check_vma=False,
    )
```

```python
import jax
import jax.numpy as jnp
from jax import lax
from jax.sharding import PartitionSpec as P

BX = 16


PRECISE = lax.Precision.HIGHEST


def padded_2(block, sides, width):
    for axis, dim in sides:
        count = lax.axis_size(axis)
        forward = [(i, i + 1) for i in range(count - 1)]
        backward = [(target, source) for source, target in forward]
        low = lax.ppermute(
            lax.slice_in_dim(block, block.shape[dim] - width, None, axis=dim), axis, forward
        )
        high = lax.ppermute(lax.slice_in_dim(block, 0, width, axis=dim), axis, backward)
        block = jnp.concatenate([low, block, high], axis=dim)
    return block


def shifted_2(value, axis, steps):
    count = lax.axis_size(axis)
    leading, last = (max(0, -steps), min(count, count - steps))
    return lax.ppermute(value, axis, [(source, source + steps) for source in range(leading, last)])


def lagrange(displace):
    position = -displace
    weights = []
    for target in range(-2, 3):
        factor = jnp.ones_like(position)
        for anchor in range(-2, 3):
            if anchor != target:
                factor = factor * ((position - anchor) / (target - anchor))
        weights.append(factor)
    return weights


def interpolate(window, across, along, span_x, span_y):
    weights_x = lagrange(across)
    weights_y = lagrange(along)
    running_total = None
    for column_tap in range(5):
        partial_sum = weights_y[0] * window[..., column_tap : column_tap + span_x, 0:span_y]
        for row_tap in range(1, 5):
            partial_sum = (
                partial_sum
                + weights_y[row_tap]
                * window[..., column_tap : column_tap + span_x, row_tap : row_tap + span_y]
            )
        tap_term = weights_x[column_tap] * partial_sum
        running_total = tap_term if running_total is None else running_total + tap_term
    return running_total


def interface_solve(packed_all, position, width):
    count = packed_all.shape[0]
    p = None
    q = None
    alphas, betas, lefts_p, lefts_q = [], [], [], []
    for j in range(count):
        first_j = packed_all[j, 0:width]
        last_j = packed_all[j, width : 2 * width]
        coef = packed_all[j, 2 * width]
        lead_left = coef[:, 0:1]
        tail_left = coef[:, 1:2]
        lead_right = coef[:, 2:3]
        tail_right = coef[:, 3:4]
        if p is None:
            pivot = jnp.ones_like(lead_left)
            alpha = first_j
            beta = -lead_right
            p_new = last_j
            q_new = -tail_right
        else:
            pivot = 1.0 + lead_left * q
            alpha = (first_j - lead_left * p) / pivot
            beta = -lead_right / pivot
            p_new = last_j - tail_left * p - tail_left * q * alpha
            q_new = -(tail_left * q * beta) - tail_right
        alphas.append(alpha)
        betas.append(beta)
        lefts_p.append(p)
        lefts_q.append(q)
        p, q = p_new, q_new
    firsts = [None] * count
    ahead = None
    for j in range(count - 1, -1, -1):
        firsts[j] = alphas[j] if ahead is None else alphas[j] + betas[j] * ahead
        ahead = firsts[j]
    zero = jnp.zeros_like(firsts[0])
    left_values = [zero] + [lefts_p[j] + lefts_q[j] * firsts[j] for j in range(1, count)]
    right_values = firsts[1:] + [zero]
    left_value = jnp.stack(left_values)[position]
    right_value = jnp.stack(right_values)[position]
    return left_value, right_value


def halo_x(block, axis, width):
    count = lax.axis_size(axis)
    forward = [(i, i + 1) for i in range(count - 1)]
    backward = [(target, source) for source, target in forward]
    low = lax.ppermute(block[:, block.shape[1] - width :], axis, forward)
    high = lax.ppermute(block[:, 0:width], axis, backward)
    return jnp.concatenate([low, block, high], axis=1)


def halo_y(block, axis, width):
    count = lax.axis_size(axis)
    forward = [(i, i + 1) for i in range(count - 1)]
    backward = [(target, source) for source, target in forward]
    low = lax.ppermute(block[:, :, block.shape[2] - width :], axis, forward)
    high = lax.ppermute(block[:, :, 0:width], axis, backward)
    return jnp.concatenate([low, high], axis=2)


def source_of(offsets, run, block_count):
    blocks = run * block_count + jnp.arange(block_count, dtype=jnp.int32)
    return blocks - lax.dynamic_slice_in_dim(offsets, run * block_count, block_count)


def slot_rank(mask):
    return jnp.cumsum(mask.astype(jnp.int32)) - 1


def local(fields, shift_x, shift_y, block_offset, group_inverse, lower_coupling, upper_coupling):
    field_count, level_count, columns, rows_here = fields.shape
    block_count = columns // BX
    window = BX + 4
    cap = 4
    channels = field_count * level_count
    count = lax.axis_size("gx")
    position = lax.axis_index("gx")
    flat = fields.reshape(channels, columns, rows_here)
    main = halo_x(flat, "gx", 2)
    halo = halo_y(main, "gy", 2).transpose(0, 2, 1)
    offsets = block_offset[:, 0]
    deltas = (-2, -1, 1, 2)
    received_main = {}
    received_halo = {}
    for delta in deltas:
        target = jnp.clip(position - delta, 0, count - 1)
        source = source_of(offsets, target, block_count)
        local_start = (source - position * block_count) * BX
        mask = (source >= position * block_count) & (source < (position + 1) * block_count)
        rank = slot_rank(mask)
        starts = [
            jnp.sum(jnp.where(mask & (rank == slot), local_start, 0)) for slot in range(cap)
        ]
        send_main = jnp.concatenate(
            [lax.dynamic_slice_in_dim(main, start, window, 1) for start in starts], axis=1
        )
        send_halo = jnp.concatenate(
            [lax.dynamic_slice_in_dim(halo, start, window, 2) for start in starts], axis=2
        )
        received_main[delta] = shifted_2(send_main, "gx", -delta)
        received_halo[delta] = shifted_2(send_halo, "gx", -delta)
    order = (-2, -1, 0, 1, 2)
    pieces_main = [main if delta == 0 else received_main[delta] for delta in order]
    pieces_halo = [halo if delta == 0 else received_halo[delta] for delta in order]
    bases = {}
    base = 0
    for delta, piece in zip(order, pieces_main):
        bases[delta] = base
        base += piece.shape[1]
    all_main = jnp.concatenate(pieces_main, axis=1)
    all_halo = jnp.concatenate(pieces_halo, axis=2)
    own_source = source_of(offsets, position, block_count)
    own_delta = own_source // block_count - position
    start_here = jnp.zeros((block_count,), jnp.int32)
    for delta in order:
        if delta == 0:
            candidate = bases[0] + (own_source - position * block_count) * BX
        else:
            rank = slot_rank(own_delta == delta)
            candidate = bases[delta] + rank * window
        start_here = jnp.where(own_delta == delta, candidate, start_here)
    window_main = jnp.stack(
        [lax.dynamic_slice_in_dim(all_main, start_here[b], window, 1) for b in range(block_count)]
    )
    window_halo = jnp.stack(
        [lax.dynamic_slice_in_dim(all_halo, start_here[b], window, 2) for b in range(block_count)]
    ).transpose(0, 1, 3, 2)
    windows = jnp.concatenate(
        [window_halo[..., 0:2], window_main, window_halo[..., 2:4]], axis=3
    ).reshape(block_count, field_count, level_count, window, rows_here + 4)
    across = shift_x.reshape(level_count, block_count, BX, rows_here).transpose(1, 0, 2, 3)[:, None]
    along = shift_y.reshape(level_count, block_count, BX, rows_here).transpose(1, 0, 2, 3)[:, None]
    interpolated = interpolate(windows, across, along, BX, rows_here)
    advected = interpolated.transpose(1, 2, 0, 3, 4).reshape(
        field_count, level_count, columns, rows_here
    )
    local_solve = jnp.einsum("lij,wljy->wliy", group_inverse, advected[0:2], precision=PRECISE)
    lower_here = lower_coupling[:, 0]
    upper_here = upper_coupling[:, 0]
    left_spike = group_inverse[:, :, 0] * lower_here[:, None]
    right_spike = group_inverse[:, :, columns - 1] * upper_here[:, None]
    coef = jnp.stack(
        [left_spike[:, 0], left_spike[:, columns - 1], right_spike[:, 0], right_spike[:, columns - 1]],
        axis=-1,
    )
    coef_rows = jnp.pad(coef, ((0, 0), (0, rows_here - 4)))
    first_row = local_solve[:, :, 0, :]
    last_row = local_solve[:, :, columns - 1, :]
    packed = jnp.concatenate([first_row, last_row, coef_rows[None]], axis=0)
    packed_all = lax.all_gather(packed, "gx")
    left_value, right_value = interface_solve(packed_all, position, first_row.shape[0])
    wind_fields = (
        local_solve
        - left_spike[None, :, :, None] * left_value[:, :, None, :]
        - right_spike[None, :, :, None] * right_value[:, :, None, :]
    )
    return (wind_fields, advected[2:4])


def solution(mesh):
    return jax.shard_map(
        local,
        mesh=mesh,
        in_specs=(
            P(None, None, "gx", "gy"),
            P(None, "gx", "gy"),
            P(None, "gx", "gy"),
            P(None, "gy"),
            P(None, "gx", None),
            P(None, "gx"),
            P(None, "gx"),
        ),
        out_specs=(P(None, None, "gx", "gy"), P(None, None, "gx", "gy")),
        check_vma=False,
    )
```

```python
import jax
import jax.numpy as jnp
from jax import lax
from jax.sharding import PartitionSpec as P

BX = 16


PRECISE = lax.Precision.HIGHEST


def padded_2(block, sides, width):
    for axis, dim in sides:
        count = lax.axis_size(axis)
        forward = [(i, i + 1) for i in range(count - 1)]
        backward = [(target, source) for source, target in forward]
        low = lax.ppermute(
            lax.slice_in_dim(block, block.shape[dim] - width, None, axis=dim), axis, forward
        )
        high = lax.ppermute(lax.slice_in_dim(block, 0, width, axis=dim), axis, backward)
        block = jnp.concatenate([low, block, high], axis=dim)
    return block


def shifted_2(value, axis, steps):
    count = lax.axis_size(axis)
    leading, last = (max(0, -steps), min(count, count - steps))
    return lax.ppermute(value, axis, [(source, source + steps) for source in range(leading, last)])


def lagrange(displace):
    position = -displace
    weights = []
    for target in range(-2, 3):
        factor = jnp.ones_like(position)
        for anchor in range(-2, 3):
            if anchor != target:
                factor = factor * ((position - anchor) / (target - anchor))
        weights.append(factor)
    return weights


def interpolate(window, across, along, span_x, span_y):
    weights_x = lagrange(across)
    weights_y = lagrange(along)
    running_total = None
    for column_tap in range(5):
        partial_sum = weights_y[0] * window[..., column_tap : column_tap + span_x, 0:span_y]
        for row_tap in range(1, 5):
            partial_sum = (
                partial_sum
                + weights_y[row_tap]
                * window[..., column_tap : column_tap + span_x, row_tap : row_tap + span_y]
            )
        tap_term = weights_x[column_tap] * partial_sum
        running_total = tap_term if running_total is None else running_total + tap_term
    return running_total


def interface_solve(packed_all, position, width):
    count = packed_all.shape[0]
    p = None
    q = None
    alphas, betas, lefts_p, lefts_q = [], [], [], []
    for j in range(count):
        first_j = packed_all[j, 0:width]
        last_j = packed_all[j, width : 2 * width]
        coef = packed_all[j, 2 * width]
        lead_left = coef[:, 0:1]
        tail_left = coef[:, 1:2]
        lead_right = coef[:, 2:3]
        tail_right = coef[:, 3:4]
        if p is None:
            pivot = jnp.ones_like(lead_left)
            alpha = first_j
            beta = -lead_right
            p_new = last_j
            q_new = -tail_right
        else:
            pivot = 1.0 + lead_left * q
            alpha = (first_j - lead_left * p) / pivot
            beta = -lead_right / pivot
            p_new = last_j - tail_left * p - tail_left * q * alpha
            q_new = -(tail_left * q * beta) - tail_right
        alphas.append(alpha)
        betas.append(beta)
        lefts_p.append(p)
        lefts_q.append(q)
        p, q = p_new, q_new
    firsts = [None] * count
    ahead = None
    for j in range(count - 1, -1, -1):
        firsts[j] = alphas[j] if ahead is None else alphas[j] + betas[j] * ahead
        ahead = firsts[j]
    zero = jnp.zeros_like(firsts[0])
    left_values = [zero] + [lefts_p[j] + lefts_q[j] * firsts[j] for j in range(1, count)]
    right_values = firsts[1:] + [zero]
    left_value = jnp.stack(left_values)[position]
    right_value = jnp.stack(right_values)[position]
    return left_value, right_value


def halo_x(block, axis, width):
    count = lax.axis_size(axis)
    forward = [(i, i + 1) for i in range(count - 1)]
    backward = [(target, source) for source, target in forward]
    low = lax.ppermute(block[:, block.shape[1] - width :], axis, forward)
    high = lax.ppermute(block[:, 0:width], axis, backward)
    return jnp.concatenate([low, block, high], axis=1)


def halo_y(block, axis, width):
    count = lax.axis_size(axis)
    forward = [(i, i + 1) for i in range(count - 1)]
    backward = [(target, source) for source, target in forward]
    low = lax.ppermute(block[:, :, block.shape[2] - width :], axis, forward)
    high = lax.ppermute(block[:, :, 0:width], axis, backward)
    return jnp.concatenate([low, high], axis=2)


def source_of(offsets, run, block_count):
    blocks = run * block_count + jnp.arange(block_count, dtype=jnp.int32)
    return blocks - lax.dynamic_slice_in_dim(offsets, run * block_count, block_count)


def slot_rank(mask):
    return jnp.cumsum(mask.astype(jnp.int32)) - 1


def send_windows(main, halo, offsets, position, count, block_count):
    window = BX + 4
    cap = 4
    channels, _, rows_here = main.shape
    deltas = (-2, -1, 1, 2)
    received_main = {}
    received_halo = {}
    for delta in deltas:
        target = jnp.clip(position - delta, 0, count - 1)
        source = source_of(offsets, target, block_count)
        local_start = (source - position * block_count) * BX
        mask = (source >= position * block_count) & (source < (position + 1) * block_count)
        rank = slot_rank(mask)
        starts = [
            jnp.sum(jnp.where(mask & (rank == slot), local_start, 0)) for slot in range(cap)
        ]
        send_main = jnp.concatenate(
            [lax.dynamic_slice_in_dim(main, start, window, 1) for start in starts], axis=1
        )
        send_halo = jnp.concatenate(
            [lax.dynamic_slice_in_dim(halo, start, window, 2) for start in starts], axis=2
        )
        span = cap * window
        send_halo = jnp.pad(send_halo, ((0, 0), (0, 0), (0, rows_here - span)))
        sent = shifted_2(jnp.concatenate([send_main, send_halo], axis=1), "gx", -delta)
        received_main[delta] = sent[:, 0:span]
        received_halo[delta] = sent[:, span:, 0:span]
    return received_main, received_halo


def assemble_windows(main, halo, received_main, received_halo, offsets, position, block_count):
    window = BX + 4
    order = (-2, -1, 0, 1, 2)
    pieces_main = [main if delta == 0 else received_main[delta] for delta in order]
    pieces_halo = [halo if delta == 0 else received_halo[delta] for delta in order]
    bases = {}
    base = 0
    for delta, piece in zip(order, pieces_main):
        bases[delta] = base
        base += piece.shape[1]
    all_main = jnp.concatenate(pieces_main, axis=1)
    all_halo = jnp.concatenate(pieces_halo, axis=2)
    own_source = source_of(offsets, position, block_count)
    own_delta = own_source // block_count - position
    start_here = jnp.zeros((block_count,), jnp.int32)
    for delta in order:
        if delta == 0:
            candidate = bases[0] + (own_source - position * block_count) * BX
        else:
            rank = slot_rank(own_delta == delta)
            candidate = bases[delta] + rank * window
        start_here = jnp.where(own_delta == delta, candidate, start_here)
    window_main = jnp.stack(
        [lax.dynamic_slice_in_dim(all_main, start_here[b], window, 1) for b in range(block_count)]
    )
    window_halo = jnp.stack(
        [lax.dynamic_slice_in_dim(all_halo, start_here[b], window, 2) for b in range(block_count)]
    ).transpose(0, 1, 3, 2)
    return jnp.concatenate(
        [window_halo[..., 0:2], window_main, window_halo[..., 2:4]], axis=3
    )


def advect_group(windows, shift_x, shift_y, field_count):
    block_count = windows.shape[0]
    level_count, columns, rows_here = shift_x.shape
    windows = windows.reshape(block_count, field_count, level_count, BX + 4, rows_here + 4)
    across = shift_x.reshape(level_count, block_count, BX, rows_here).transpose(1, 0, 2, 3)[:, None]
    along = shift_y.reshape(level_count, block_count, BX, rows_here).transpose(1, 0, 2, 3)[:, None]
    interpolated = interpolate(windows, across, along, BX, rows_here)
    return interpolated.transpose(1, 2, 0, 3, 4).reshape(
        field_count, level_count, columns, rows_here
    )


def local(fields, shift_x, shift_y, block_offset, group_inverse, lower_coupling, upper_coupling):
    field_count, level_count, columns, rows_here = fields.shape
    block_count = columns // BX
    channels = field_count * level_count
    wind_channels = 2 * level_count
    count = lax.axis_size("gx")
    position = lax.axis_index("gx")
    flat = fields.reshape(channels, columns, rows_here)
    main = halo_x(flat, "gx", 2)
    halo = halo_y(main, "gy", 2).transpose(0, 2, 1)
    offsets = block_offset[:, 0]
    wind_main, wind_halo = main[:wind_channels], halo[:wind_channels]
    tracer_main, tracer_halo = main[wind_channels:], halo[wind_channels:]
    wind_received = send_windows(wind_main, wind_halo, offsets, position, count, block_count)
    tracer_received = send_windows(tracer_main, tracer_halo, offsets, position, count, block_count)
    wind_windows = assemble_windows(
        wind_main, wind_halo, *wind_received, offsets, position, block_count
    )
    winds = advect_group(wind_windows, shift_x, shift_y, 2)
    local_solve = jnp.einsum("lij,wljy->wliy", group_inverse, winds, precision=PRECISE)
    lower_here = lower_coupling[:, 0]
    upper_here = upper_coupling[:, 0]
    left_spike = group_inverse[:, :, 0] * lower_here[:, None]
    right_spike = group_inverse[:, :, columns - 1] * upper_here[:, None]
    coef = jnp.stack(
        [left_spike[:, 0], left_spike[:, columns - 1], right_spike[:, 0], right_spike[:, columns - 1]],
        axis=-1,
    )
    coef_rows = jnp.pad(coef, ((0, 0), (0, rows_here - 4)))
    first_row = local_solve[:, :, 0, :]
    last_row = local_solve[:, :, columns - 1, :]
    packed = jnp.concatenate([first_row, last_row, coef_rows[None]], axis=0)
    packed_all = lax.all_gather(packed, "gx")
    packed_all, tracer_received = lax.optimization_barrier((packed_all, tracer_received))
    left_value, right_value = interface_solve(packed_all, position, first_row.shape[0])
    wind_fields = (
        local_solve
        - left_spike[None, :, :, None] * left_value[:, :, None, :]
        - right_spike[None, :, :, None] * right_value[:, :, None, :]
    )
    tracer_windows = assemble_windows(
        tracer_main, tracer_halo, *tracer_received, offsets, position, block_count
    )
    tracers = advect_group(tracer_windows, shift_x, shift_y, field_count - 2)
    return (wind_fields, tracers)


def solution(mesh):
    return jax.shard_map(
        local,
        mesh=mesh,
        in_specs=(
            P(None, None, "gx", "gy"),
            P(None, "gx", "gy"),
            P(None, "gx", "gy"),
            P(None, "gy"),
            P(None, "gx", None),
            P(None, "gx"),
            P(None, "gx"),
        ),
        out_specs=(P(None, None, "gx", "gy"), P(None, None, "gx", "gy")),
        check_vma=False,
    )
```

```python
import jax
import jax.numpy as jnp
from jax import lax
from jax.sharding import PartitionSpec as P

BX = 16


PRECISE = lax.Precision.HIGHEST


def padded_2(block, sides, width):
    for axis, dim in sides:
        count = lax.axis_size(axis)
        forward = [(i, i + 1) for i in range(count - 1)]
        backward = [(target, source) for source, target in forward]
        low = lax.ppermute(
            lax.slice_in_dim(block, block.shape[dim] - width, None, axis=dim), axis, forward
        )
        high = lax.ppermute(lax.slice_in_dim(block, 0, width, axis=dim), axis, backward)
        block = jnp.concatenate([low, block, high], axis=dim)
    return block


def shifted_2(value, axis, steps):
    count = lax.axis_size(axis)
    leading, last = (max(0, -steps), min(count, count - steps))
    return lax.ppermute(value, axis, [(source, source + steps) for source in range(leading, last)])


def lagrange(displace):
    position = -displace
    weights = []
    for target in range(-2, 3):
        factor = jnp.ones_like(position)
        for anchor in range(-2, 3):
            if anchor != target:
                factor = factor * ((position - anchor) / (target - anchor))
        weights.append(factor)
    return weights


def interpolate(window, across, along, span_x, span_y):
    weights_x = lagrange(across)
    weights_y = lagrange(along)
    running_total = None
    for column_tap in range(5):
        partial_sum = weights_y[0] * window[..., column_tap : column_tap + span_x, 0:span_y]
        for row_tap in range(1, 5):
            partial_sum = (
                partial_sum
                + weights_y[row_tap]
                * window[..., column_tap : column_tap + span_x, row_tap : row_tap + span_y]
            )
        tap_term = weights_x[column_tap] * partial_sum
        running_total = tap_term if running_total is None else running_total + tap_term
    return running_total


def interface_solve(packed_all, position, width):
    count = packed_all.shape[0]
    p = None
    q = None
    alphas, betas, lefts_p, lefts_q = [], [], [], []
    for j in range(count):
        first_j = packed_all[j, 0:width]
        last_j = packed_all[j, width : 2 * width]
        coef = packed_all[j, 2 * width]
        lead_left = coef[:, 0:1]
        tail_left = coef[:, 1:2]
        lead_right = coef[:, 2:3]
        tail_right = coef[:, 3:4]
        if p is None:
            pivot = jnp.ones_like(lead_left)
            alpha = first_j
            beta = -lead_right
            p_new = last_j
            q_new = -tail_right
        else:
            pivot = 1.0 + lead_left * q
            alpha = (first_j - lead_left * p) / pivot
            beta = -lead_right / pivot
            p_new = last_j - tail_left * p - tail_left * q * alpha
            q_new = -(tail_left * q * beta) - tail_right
        alphas.append(alpha)
        betas.append(beta)
        lefts_p.append(p)
        lefts_q.append(q)
        p, q = p_new, q_new
    firsts = [None] * count
    ahead = None
    for j in range(count - 1, -1, -1):
        firsts[j] = alphas[j] if ahead is None else alphas[j] + betas[j] * ahead
        ahead = firsts[j]
    zero = jnp.zeros_like(firsts[0])
    left_values = [zero] + [lefts_p[j] + lefts_q[j] * firsts[j] for j in range(1, count)]
    right_values = firsts[1:] + [zero]
    left_value = jnp.stack(left_values)[position]
    right_value = jnp.stack(right_values)[position]
    return left_value, right_value


def halo_x(block, axis, width):
    count = lax.axis_size(axis)
    forward = [(i, i + 1) for i in range(count - 1)]
    backward = [(target, source) for source, target in forward]
    low = lax.ppermute(block[:, block.shape[1] - width :], axis, forward)
    high = lax.ppermute(block[:, 0:width], axis, backward)
    return jnp.concatenate([low, block, high], axis=1)


def halo_y(block, axis, width):
    count = lax.axis_size(axis)
    forward = [(i, i + 1) for i in range(count - 1)]
    backward = [(target, source) for source, target in forward]
    low = lax.ppermute(block[:, :, block.shape[2] - width :], axis, forward)
    high = lax.ppermute(block[:, :, 0:width], axis, backward)
    return jnp.concatenate([low, high], axis=2)


def source_of(offsets, run, block_count):
    blocks = run * block_count + jnp.arange(block_count, dtype=jnp.int32)
    return blocks - lax.dynamic_slice_in_dim(offsets, run * block_count, block_count)


def slot_rank(mask):
    return jnp.cumsum(mask.astype(jnp.int32)) - 1


def send_windows(main, halo, offsets, position, count, block_count):
    window = BX + 4
    cap = 4
    channels, _, rows_here = main.shape
    deltas = (-2, -1, 1, 2)
    received_main = {}
    received_halo = {}
    for delta in deltas:
        target = jnp.clip(position - delta, 0, count - 1)
        source = source_of(offsets, target, block_count)
        local_start = (source - position * block_count) * BX
        mask = (source >= position * block_count) & (source < (position + 1) * block_count)
        rank = slot_rank(mask)
        starts = [
            jnp.sum(jnp.where(mask & (rank == slot), local_start, 0)) for slot in range(cap)
        ]
        send_main = jnp.concatenate(
            [lax.dynamic_slice_in_dim(main, start, window, 1) for start in starts], axis=1
        )
        send_halo = jnp.concatenate(
            [lax.dynamic_slice_in_dim(halo, start, window, 2) for start in starts], axis=2
        )
        span = cap * window
        send_halo = jnp.pad(send_halo, ((0, 0), (0, 0), (0, rows_here - span)))
        sent = shifted_2(jnp.concatenate([send_main, send_halo], axis=1), "gx", -delta)
        received_main[delta] = sent[:, 0:span]
        received_halo[delta] = sent[:, span:, 0:span]
    return received_main, received_halo


def assemble_windows(main, halo, received_main, received_halo, offsets, position, block_count):
    window = BX + 4
    order = (-2, -1, 0, 1, 2)
    pieces_main = [main if delta == 0 else received_main[delta] for delta in order]
    pieces_halo = [halo if delta == 0 else received_halo[delta] for delta in order]
    bases = {}
    base = 0
    for delta, piece in zip(order, pieces_main):
        bases[delta] = base
        base += piece.shape[1]
    all_main = jnp.concatenate(pieces_main, axis=1)
    all_halo = jnp.concatenate(pieces_halo, axis=2)
    own_source = source_of(offsets, position, block_count)
    own_delta = own_source // block_count - position
    start_here = jnp.zeros((block_count,), jnp.int32)
    for delta in order:
        if delta == 0:
            candidate = bases[0] + (own_source - position * block_count) * BX
        else:
            rank = slot_rank(own_delta == delta)
            candidate = bases[delta] + rank * window
        start_here = jnp.where(own_delta == delta, candidate, start_here)
    window_main = jnp.stack(
        [lax.dynamic_slice_in_dim(all_main, start_here[b], window, 1) for b in range(block_count)]
    )
    window_halo = jnp.stack(
        [lax.dynamic_slice_in_dim(all_halo, start_here[b], window, 2) for b in range(block_count)]
    ).transpose(0, 1, 3, 2)
    return jnp.concatenate(
        [window_halo[..., 0:2], window_main, window_halo[..., 2:4]], axis=3
    )


def advect_group(windows, shift_x, shift_y, field_count):
    block_count = windows.shape[0]
    level_count, columns, rows_here = shift_x.shape
    windows = windows.reshape(block_count, field_count, level_count, BX + 4, rows_here + 4)
    across = shift_x.reshape(level_count, block_count, BX, rows_here).transpose(1, 0, 2, 3)[:, None]
    along = shift_y.reshape(level_count, block_count, BX, rows_here).transpose(1, 0, 2, 3)[:, None]
    interpolated = interpolate(windows, across, along, BX, rows_here)
    return interpolated.transpose(1, 2, 0, 3, 4).reshape(
        field_count, level_count, columns, rows_here
    )


def local(fields, shift_x, shift_y, block_offset, group_inverse, lower_coupling, upper_coupling):
    field_count, level_count, columns, rows_here = fields.shape
    block_count = columns // BX
    channels = field_count * level_count
    wind_channels = 2 * level_count
    count = lax.axis_size("gx")
    position = lax.axis_index("gx")
    flat = fields.reshape(channels, columns, rows_here)
    main = halo_x(flat, "gx", 2)
    halo = halo_y(main, "gy", 2).transpose(0, 2, 1)
    offsets = block_offset[:, 0]
    wind_main, wind_halo = main[:wind_channels], halo[:wind_channels]
    tracer_main, tracer_halo = main[wind_channels:], halo[wind_channels:]
    wind_received = send_windows(wind_main, wind_halo, offsets, position, count, block_count)
    tracer_received = send_windows(tracer_main, tracer_halo, offsets, position, count, block_count)
    wind_windows = assemble_windows(
        wind_main, wind_halo, *wind_received, offsets, position, block_count
    )
    winds = advect_group(wind_windows, shift_x, shift_y, 2)
    local_solve = jnp.einsum("lij,wljy->wliy", group_inverse, winds, precision=PRECISE)
    lower_here = lower_coupling[:, 0]
    upper_here = upper_coupling[:, 0]
    left_spike = group_inverse[:, :, 0] * lower_here[:, None]
    right_spike = group_inverse[:, :, columns - 1] * upper_here[:, None]
    coef = jnp.stack(
        [left_spike[:, 0], left_spike[:, columns - 1], right_spike[:, 0], right_spike[:, columns - 1]],
        axis=-1,
    )
    coef_rows = jnp.pad(coef, ((0, 0), (0, rows_here - 4)))
    first_row = local_solve[:, :, 0, :]
    last_row = local_solve[:, :, columns - 1, :]
    packed = jnp.concatenate([first_row, last_row, coef_rows[None]], axis=0)
    held = packed[None]
    step = 1
    while step < count:
        ring = [(i, (i + step) % count) for i in range(count)]
        held = jnp.concatenate([held, lax.ppermute(held, "gx", ring)], axis=0)
        if step == 1:
            held, tracer_received = lax.optimization_barrier((held, tracer_received))
        step *= 2
    reverse = held[::-1]
    doubled = jnp.concatenate([reverse, reverse], axis=0)
    packed_all = lax.dynamic_slice_in_dim(doubled, count - 1 - position, count, 0)
    left_value, right_value = interface_solve(packed_all, position, first_row.shape[0])
    wind_fields = (
        local_solve
        - left_spike[None, :, :, None] * left_value[:, :, None, :]
        - right_spike[None, :, :, None] * right_value[:, :, None, :]
    )
    tracer_windows = assemble_windows(
        tracer_main, tracer_halo, *tracer_received, offsets, position, block_count
    )
    tracers = advect_group(tracer_windows, shift_x, shift_y, field_count - 2)
    return (wind_fields, tracers)


def solution(mesh):
    return jax.shard_map(
        local,
        mesh=mesh,
        in_specs=(
            P(None, None, "gx", "gy"),
            P(None, "gx", "gy"),
            P(None, "gx", "gy"),
            P(None, "gy"),
            P(None, "gx", None),
            P(None, "gx"),
            P(None, "gx"),
        ),
        out_specs=(P(None, None, "gx", "gy"), P(None, None, "gx", "gy")),
        check_vma=False,
    )
```

```python
import jax
import jax.numpy as jnp
from jax import lax
from jax.sharding import PartitionSpec as P
from jax.experimental import pallas as pl
from jax.experimental.pallas import tpu as pltpu

BX = 16


PRECISE = lax.Precision.HIGHEST


def padded_2(block, sides, width):
    for axis, dim in sides:
        count = lax.axis_size(axis)
        forward = [(i, i + 1) for i in range(count - 1)]
        backward = [(target, source) for source, target in forward]
        low = lax.ppermute(
            lax.slice_in_dim(block, block.shape[dim] - width, None, axis=dim), axis, forward
        )
        high = lax.ppermute(lax.slice_in_dim(block, 0, width, axis=dim), axis, backward)
        block = jnp.concatenate([low, block, high], axis=dim)
    return block


def shifted_2(value, axis, steps):
    count = lax.axis_size(axis)
    leading, last = (max(0, -steps), min(count, count - steps))
    return lax.ppermute(value, axis, [(source, source + steps) for source in range(leading, last)])


def lagrange(displace):
    position = -displace
    weights = []
    for target in range(-2, 3):
        factor = jnp.ones_like(position)
        for anchor in range(-2, 3):
            if anchor != target:
                factor = factor * ((position - anchor) / (target - anchor))
        weights.append(factor)
    return weights


def interpolate(window, across, along, span_x, span_y):
    weights_x = lagrange(across)
    weights_y = lagrange(along)
    running_total = None
    for column_tap in range(5):
        partial_sum = weights_y[0] * window[..., column_tap : column_tap + span_x, 0:span_y]
        for row_tap in range(1, 5):
            partial_sum = (
                partial_sum
                + weights_y[row_tap]
                * window[..., column_tap : column_tap + span_x, row_tap : row_tap + span_y]
            )
        tap_term = weights_x[column_tap] * partial_sum
        running_total = tap_term if running_total is None else running_total + tap_term
    return running_total


def _solve_body(pos_ref, packed_ref, left_ref, right_ref, alpha_s, beta_s, p_s, q_s, f_s):
    count = packed_ref.shape[0]
    width = left_ref.shape[0]
    levels, lanes = left_ref.shape[1], left_ref.shape[2]
    p = jnp.zeros((width, levels, lanes), jnp.float32)
    q = jnp.zeros((levels, lanes), jnp.float32)
    for j in range(count):
        first = packed_ref[j, 0:width]
        last = packed_ref[j, width : 2 * width]
        coef = packed_ref[j, 2 * width]
        lead_left = jnp.broadcast_to(coef[:, 0:1], (levels, lanes))
        tail_left = jnp.broadcast_to(coef[:, 1:2], (levels, lanes))
        lead_right = jnp.broadcast_to(coef[:, 2:3], (levels, lanes))
        tail_right = jnp.broadcast_to(coef[:, 3:4], (levels, lanes))
        pivot = 1.0 + lead_left * q
        alpha = (first - lead_left * p) / pivot
        beta = -lead_right / pivot
        p_s[j] = p
        q_s[j] = q
        alpha_s[j] = alpha
        beta_s[j] = beta
        p = last - tail_left * p - tail_left * q * alpha
        q = -(tail_left * q * beta) - tail_right
    ahead = jnp.zeros((width, levels, lanes), jnp.float32)
    f_s[count] = ahead
    for j in range(count - 1, -1, -1):
        ahead = alpha_s[j] + beta_s[j] * ahead
        f_s[j] = ahead
    pos = pos_ref[0]
    left_ref[...] = p_s[pos] + q_s[pos] * f_s[pos]
    right_ref[...] = f_s[pos + 1]

def interface_solve(packed_all, position, width):
    count, _, levels, lanes = packed_all.shape
    out = jax.ShapeDtypeStruct((width, levels, lanes), jnp.float32)
    vmem = pltpu.VMEM
    return pl.pallas_call(
        _solve_body,
        out_shape=(out, out),
        in_specs=[pl.BlockSpec(memory_space=pltpu.SMEM), pl.BlockSpec(memory_space=vmem)],
        out_specs=(pl.BlockSpec(memory_space=vmem), pl.BlockSpec(memory_space=vmem)),
        scratch_shapes=[
            pltpu.VMEM((count, width, levels, lanes), jnp.float32),
            pltpu.VMEM((count, levels, lanes), jnp.float32),
            pltpu.VMEM((count, width, levels, lanes), jnp.float32),
            pltpu.VMEM((count, levels, lanes), jnp.float32),
            pltpu.VMEM((count + 1, width, levels, lanes), jnp.float32),
        ],
    )(jnp.reshape(position, (1,)).astype(jnp.int32), packed_all)


def halo_x(block, axis, width):
    count = lax.axis_size(axis)
    forward = [(i, i + 1) for i in range(count - 1)]
    backward = [(target, source) for source, target in forward]
    low = lax.ppermute(block[:, block.shape[1] - width :], axis, forward)
    high = lax.ppermute(block[:, 0:width], axis, backward)
    return jnp.concatenate([low, block, high], axis=1)


def halo_y(block, axis, width):
    count = lax.axis_size(axis)
    forward = [(i, i + 1) for i in range(count - 1)]
    backward = [(target, source) for source, target in forward]
    low = lax.ppermute(block[:, :, block.shape[2] - width :], axis, forward)
    high = lax.ppermute(block[:, :, 0:width], axis, backward)
    return jnp.concatenate([low, high], axis=2)


def source_of(offsets, run, block_count):
    blocks = run * block_count + jnp.arange(block_count, dtype=jnp.int32)
    return blocks - lax.dynamic_slice_in_dim(offsets, run * block_count, block_count)


def slot_rank(mask):
    return jnp.cumsum(mask.astype(jnp.int32)) - 1


def send_windows(main, halo, offsets, position, count, block_count):
    window = BX + 4
    cap = 4
    channels, _, rows_here = main.shape
    deltas = (-2, -1, 1, 2)
    received_main = {}
    received_halo = {}
    for delta in deltas:
        target = jnp.clip(position - delta, 0, count - 1)
        source = source_of(offsets, target, block_count)
        local_start = (source - position * block_count) * BX
        mask = (source >= position * block_count) & (source < (position + 1) * block_count)
        rank = slot_rank(mask)
        starts = [
            jnp.sum(jnp.where(mask & (rank == slot), local_start, 0)) for slot in range(cap)
        ]
        send_main = jnp.concatenate(
            [lax.dynamic_slice_in_dim(main, start, window, 1) for start in starts], axis=1
        )
        send_halo = jnp.concatenate(
            [lax.dynamic_slice_in_dim(halo, start, window, 2) for start in starts], axis=2
        )
        span = cap * window
        send_halo = jnp.pad(send_halo, ((0, 0), (0, 0), (0, rows_here - span)))
        sent = shifted_2(jnp.concatenate([send_main, send_halo], axis=1), "gx", -delta)
        received_main[delta] = sent[:, 0:span]
        received_halo[delta] = sent[:, span:, 0:span]
    return received_main, received_halo


def assemble_windows(main, halo, received_main, received_halo, offsets, position, block_count):
    window = BX + 4
    order = (-2, -1, 0, 1, 2)
    pieces_main = [main if delta == 0 else received_main[delta] for delta in order]
    pieces_halo = [halo if delta == 0 else received_halo[delta] for delta in order]
    bases = {}
    base = 0
    for delta, piece in zip(order, pieces_main):
        bases[delta] = base
        base += piece.shape[1]
    all_main = jnp.concatenate(pieces_main, axis=1)
    all_halo = jnp.concatenate(pieces_halo, axis=2)
    own_source = source_of(offsets, position, block_count)
    own_delta = own_source // block_count - position
    start_here = jnp.zeros((block_count,), jnp.int32)
    for delta in order:
        if delta == 0:
            candidate = bases[0] + (own_source - position * block_count) * BX
        else:
            rank = slot_rank(own_delta == delta)
            candidate = bases[delta] + rank * window
        start_here = jnp.where(own_delta == delta, candidate, start_here)
    window_main = jnp.stack(
        [lax.dynamic_slice_in_dim(all_main, start_here[b], window, 1) for b in range(block_count)]
    )
    window_halo = jnp.stack(
        [lax.dynamic_slice_in_dim(all_halo, start_here[b], window, 2) for b in range(block_count)]
    ).transpose(0, 1, 3, 2)
    return jnp.concatenate(
        [window_halo[..., 0:2], window_main, window_halo[..., 2:4]], axis=3
    )


def advect_group(windows, shift_x, shift_y, field_count):
    block_count = windows.shape[0]
    level_count, columns, rows_here = shift_x.shape
    windows = windows.reshape(block_count, field_count, level_count, BX + 4, rows_here + 4)
    across = shift_x.reshape(level_count, block_count, BX, rows_here).transpose(1, 0, 2, 3)[:, None]
    along = shift_y.reshape(level_count, block_count, BX, rows_here).transpose(1, 0, 2, 3)[:, None]
    interpolated = interpolate(windows, across, along, BX, rows_here)
    return interpolated.transpose(1, 2, 0, 3, 4).reshape(
        field_count, level_count, columns, rows_here
    )


def local(fields, shift_x, shift_y, block_offset, group_inverse, lower_coupling, upper_coupling):
    field_count, level_count, columns, rows_here = fields.shape
    block_count = columns // BX
    channels = field_count * level_count
    wind_channels = 2 * level_count
    count = lax.axis_size("gx")
    position = lax.axis_index("gx")
    flat = fields.reshape(channels, columns, rows_here)
    main = halo_x(flat, "gx", 2)
    halo = halo_y(main, "gy", 2).transpose(0, 2, 1)
    offsets = block_offset[:, 0]
    wind_main, wind_halo = main[:wind_channels], halo[:wind_channels]
    tracer_main, tracer_halo = main[wind_channels:], halo[wind_channels:]
    wind_received = send_windows(wind_main, wind_halo, offsets, position, count, block_count)
    tracer_received = send_windows(tracer_main, tracer_halo, offsets, position, count, block_count)
    wind_windows = assemble_windows(
        wind_main, wind_halo, *wind_received, offsets, position, block_count
    )
    winds = advect_group(wind_windows, shift_x, shift_y, 2)
    local_solve = jnp.einsum("lij,wljy->wliy", group_inverse, winds, precision=PRECISE)
    lower_here = lower_coupling[:, 0]
    upper_here = upper_coupling[:, 0]
    left_spike = group_inverse[:, :, 0] * lower_here[:, None]
    right_spike = group_inverse[:, :, columns - 1] * upper_here[:, None]
    coef = jnp.stack(
        [left_spike[:, 0], left_spike[:, columns - 1], right_spike[:, 0], right_spike[:, columns - 1]],
        axis=-1,
    )
    coef_rows = jnp.pad(coef, ((0, 0), (0, rows_here - 4)))
    first_row = local_solve[:, :, 0, :]
    last_row = local_solve[:, :, columns - 1, :]
    packed = jnp.concatenate([first_row, last_row, coef_rows[None]], axis=0)
    held = packed[None]
    step = 1
    while step < count:
        ring = [(i, (i + step) % count) for i in range(count)]
        held = jnp.concatenate([held, lax.ppermute(held, "gx", ring)], axis=0)
        if step == 1:
            held, tracer_received = lax.optimization_barrier((held, tracer_received))
        step *= 2
    reverse = held[::-1]
    doubled = jnp.concatenate([reverse, reverse], axis=0)
    packed_all = lax.dynamic_slice_in_dim(doubled, count - 1 - position, count, 0)
    left_value, right_value = interface_solve(packed_all, position, first_row.shape[0])
    wind_fields = (
        local_solve
        - left_spike[None, :, :, None] * left_value[:, :, None, :]
        - right_spike[None, :, :, None] * right_value[:, :, None, :]
    )
    tracer_windows = assemble_windows(
        tracer_main, tracer_halo, *tracer_received, offsets, position, block_count
    )
    tracers = advect_group(tracer_windows, shift_x, shift_y, field_count - 2)
    return (wind_fields, tracers)


def solution(mesh):
    return jax.shard_map(
        local,
        mesh=mesh,
        in_specs=(
            P(None, None, "gx", "gy"),
            P(None, "gx", "gy"),
            P(None, "gx", "gy"),
            P(None, "gy"),
            P(None, "gx", None),
            P(None, "gx"),
            P(None, "gx"),
        ),
        out_specs=(P(None, None, "gx", "gy"), P(None, None, "gx", "gy")),
        check_vma=False,
    )
```

```python
import jax
import jax.numpy as jnp
from jax import lax
from jax.sharding import PartitionSpec as P
from jax.experimental import pallas as pl
from jax.experimental.pallas import tpu as pltpu

BX = 16


PRECISE = lax.Precision.HIGHEST


def padded_2(block, sides, width):
    for axis, dim in sides:
        count = lax.axis_size(axis)
        forward = [(i, i + 1) for i in range(count - 1)]
        backward = [(target, source) for source, target in forward]
        low = lax.ppermute(
            lax.slice_in_dim(block, block.shape[dim] - width, None, axis=dim), axis, forward
        )
        high = lax.ppermute(lax.slice_in_dim(block, 0, width, axis=dim), axis, backward)
        block = jnp.concatenate([low, block, high], axis=dim)
    return block


def shifted_2(value, axis, steps):
    count = lax.axis_size(axis)
    leading, last = (max(0, -steps), min(count, count - steps))
    return lax.ppermute(value, axis, [(source, source + steps) for source in range(leading, last)])


def lagrange(displace):
    position = -displace
    weights = []
    for target in range(-2, 3):
        factor = jnp.ones_like(position)
        for anchor in range(-2, 3):
            if anchor != target:
                factor = factor * ((position - anchor) / (target - anchor))
        weights.append(factor)
    return weights


def interpolate(window, across, along, span_x, span_y):
    weights_x = lagrange(across)
    weights_y = lagrange(along)
    running_total = None
    for column_tap in range(5):
        partial_sum = weights_y[0] * window[..., column_tap : column_tap + span_x, 0:span_y]
        for row_tap in range(1, 5):
            partial_sum = (
                partial_sum
                + weights_y[row_tap]
                * window[..., column_tap : column_tap + span_x, row_tap : row_tap + span_y]
            )
        tap_term = weights_x[column_tap] * partial_sum
        running_total = tap_term if running_total is None else running_total + tap_term
    return running_total


def _solve_body(pos_ref, packed_ref, left_ref, right_ref, alpha_s, beta_s, p_s, q_s, f_s):
    count = packed_ref.shape[0]
    width = left_ref.shape[0]
    levels, lanes = left_ref.shape[1], left_ref.shape[2]
    p = jnp.zeros((width, levels, lanes), jnp.float32)
    q = jnp.zeros((levels, lanes), jnp.float32)
    for j in range(count):
        first = packed_ref[j, 0:width]
        last = packed_ref[j, width : 2 * width]
        coef = packed_ref[j, 2 * width]
        lead_left = jnp.broadcast_to(coef[:, 0:1], (levels, lanes))
        tail_left = jnp.broadcast_to(coef[:, 1:2], (levels, lanes))
        lead_right = jnp.broadcast_to(coef[:, 2:3], (levels, lanes))
        tail_right = jnp.broadcast_to(coef[:, 3:4], (levels, lanes))
        pivot = 1.0 + lead_left * q
        alpha = (first - lead_left * p) / pivot
        beta = -lead_right / pivot
        p_s[j] = p
        q_s[j] = q
        alpha_s[j] = alpha
        beta_s[j] = beta
        p = last - tail_left * p - tail_left * q * alpha
        q = -(tail_left * q * beta) - tail_right
    ahead = jnp.zeros((width, levels, lanes), jnp.float32)
    f_s[count] = ahead
    for j in range(count - 1, -1, -1):
        ahead = alpha_s[j] + beta_s[j] * ahead
        f_s[j] = ahead
    pos = pos_ref[0]
    left_ref[...] = p_s[pos] + q_s[pos] * f_s[pos]
    right_ref[...] = f_s[pos + 1]

def interface_solve(packed_all, position, width):
    count, _, levels, lanes = packed_all.shape
    out = jax.ShapeDtypeStruct((width, levels, lanes), jnp.float32)
    vmem = pltpu.VMEM
    return pl.pallas_call(
        _solve_body,
        out_shape=(out, out),
        in_specs=[pl.BlockSpec(memory_space=pltpu.SMEM), pl.BlockSpec(memory_space=vmem)],
        out_specs=(pl.BlockSpec(memory_space=vmem), pl.BlockSpec(memory_space=vmem)),
        scratch_shapes=[
            pltpu.VMEM((count, width, levels, lanes), jnp.float32),
            pltpu.VMEM((count, levels, lanes), jnp.float32),
            pltpu.VMEM((count, width, levels, lanes), jnp.float32),
            pltpu.VMEM((count, levels, lanes), jnp.float32),
            pltpu.VMEM((count + 1, width, levels, lanes), jnp.float32),
        ],
    )(jnp.reshape(position, (1,)).astype(jnp.int32), packed_all)


def halo_x(block, axis, width):
    count = lax.axis_size(axis)
    forward = [(i, i + 1) for i in range(count - 1)]
    backward = [(target, source) for source, target in forward]
    low = lax.ppermute(block[:, block.shape[1] - width :], axis, forward)
    high = lax.ppermute(block[:, 0:width], axis, backward)
    return jnp.concatenate([low, block, high], axis=1)


def halo_y(block, axis, width):
    count = lax.axis_size(axis)
    forward = [(i, i + 1) for i in range(count - 1)]
    backward = [(target, source) for source, target in forward]
    low = lax.ppermute(block[:, :, block.shape[2] - width :], axis, forward)
    high = lax.ppermute(block[:, :, 0:width], axis, backward)
    return jnp.concatenate([low, high], axis=2)


def source_of(offsets, run, block_count):
    blocks = run * block_count + jnp.arange(block_count, dtype=jnp.int32)
    return blocks - lax.dynamic_slice_in_dim(offsets, run * block_count, block_count)


def slot_rank(mask):
    return jnp.cumsum(mask.astype(jnp.int32)) - 1


def send_windows(main, halo, offsets, position, count, block_count):
    window = BX + 4
    cap = 4
    channels, _, rows_here = main.shape
    deltas = (-2, -1, 1, 2)
    received_main = {}
    received_halo = {}
    for delta in deltas:
        target = jnp.clip(position - delta, 0, count - 1)
        source = source_of(offsets, target, block_count)
        local_start = (source - position * block_count) * BX
        mask = (source >= position * block_count) & (source < (position + 1) * block_count)
        rank = slot_rank(mask)
        starts = [
            jnp.sum(jnp.where(mask & (rank == slot), local_start, 0)) for slot in range(cap)
        ]
        send_main = jnp.concatenate(
            [lax.dynamic_slice_in_dim(main, start, window, 1) for start in starts], axis=1
        )
        send_halo = jnp.concatenate(
            [lax.dynamic_slice_in_dim(halo, start, window, 2) for start in starts], axis=2
        )
        span = cap * window
        send_halo = jnp.pad(send_halo, ((0, 0), (0, 0), (0, rows_here - span)))
        sent = shifted_2(jnp.concatenate([send_main, send_halo], axis=1), "gx", -delta)
        received_main[delta] = sent[:, 0:span]
        received_halo[delta] = sent[:, span:, 0:span]
    return received_main, received_halo


def assemble_windows(main, halo, received_main, received_halo, offsets, position, block_count):
    window = BX + 4
    order = (-2, -1, 0, 1, 2)
    pieces_main = [main if delta == 0 else received_main[delta] for delta in order]
    pieces_halo = [halo if delta == 0 else received_halo[delta] for delta in order]
    bases = {}
    base = 0
    for delta, piece in zip(order, pieces_main):
        bases[delta] = base
        base += piece.shape[1]
    all_main = jnp.concatenate(pieces_main, axis=1)
    all_halo = jnp.concatenate(pieces_halo, axis=2)
    own_source = source_of(offsets, position, block_count)
    own_delta = own_source // block_count - position
    start_here = jnp.zeros((block_count,), jnp.int32)
    for delta in order:
        if delta == 0:
            candidate = bases[0] + (own_source - position * block_count) * BX
        else:
            rank = slot_rank(own_delta == delta)
            candidate = bases[delta] + rank * window
        start_here = jnp.where(own_delta == delta, candidate, start_here)
    window_main = jnp.stack(
        [lax.dynamic_slice_in_dim(all_main, start_here[b], window, 1) for b in range(block_count)]
    )
    window_halo = jnp.stack(
        [lax.dynamic_slice_in_dim(all_halo, start_here[b], window, 2) for b in range(block_count)]
    ).transpose(0, 1, 3, 2)
    return jnp.concatenate(
        [window_halo[..., 0:2], window_main, window_halo[..., 2:4]], axis=3
    )


def advect_group(windows, shift_x, shift_y, field_count):
    block_count = windows.shape[0]
    level_count, columns, rows_here = shift_x.shape
    windows = windows.reshape(block_count, field_count, level_count, BX + 4, rows_here + 4)
    across = shift_x.reshape(level_count, block_count, BX, rows_here).transpose(1, 0, 2, 3)[:, None]
    along = shift_y.reshape(level_count, block_count, BX, rows_here).transpose(1, 0, 2, 3)[:, None]
    interpolated = interpolate(windows, across, along, BX, rows_here)
    return interpolated.transpose(1, 2, 0, 3, 4).reshape(
        field_count, level_count, columns, rows_here
    )


def local(fields, shift_x, shift_y, block_offset, group_inverse, lower_coupling, upper_coupling):
    field_count, level_count, columns, rows_here = fields.shape
    block_count = columns // BX
    channels = field_count * level_count
    wind_channels = 2 * level_count
    count = lax.axis_size("gx")
    position = lax.axis_index("gx")
    flat = fields.reshape(channels, columns, rows_here)
    main = halo_x(flat, "gx", 2)
    halo = halo_y(main, "gy", 2).transpose(0, 2, 1)
    offsets = block_offset[:, 0]
    wind_main, wind_halo = main[:wind_channels], halo[:wind_channels]
    tracer_main, tracer_halo = main[wind_channels:], halo[wind_channels:]
    wind_received = send_windows(wind_main, wind_halo, offsets, position, count, block_count)
    tracer_received = send_windows(tracer_main, tracer_halo, offsets, position, count, block_count)
    wind_windows = assemble_windows(
        wind_main, wind_halo, *wind_received, offsets, position, block_count
    )
    winds = advect_group(wind_windows, shift_x, shift_y, 2)
    local_solve = jnp.einsum("lij,wljy->wliy", group_inverse, winds, precision=PRECISE)
    lower_here = lower_coupling[:, 0]
    upper_here = upper_coupling[:, 0]
    left_spike = group_inverse[:, :, 0] * lower_here[:, None]
    right_spike = group_inverse[:, :, columns - 1] * upper_here[:, None]
    coef = jnp.stack(
        [left_spike[:, 0], left_spike[:, columns - 1], right_spike[:, 0], right_spike[:, columns - 1]],
        axis=-1,
    )
    coef_rows = jnp.pad(coef, ((0, 0), (0, rows_here - 4)))
    first_row = local_solve[:, :, 0, :]
    last_row = local_solve[:, :, columns - 1, :]
    packed = jnp.concatenate([first_row, last_row, coef_rows[None]], axis=0)
    held = packed[None]
    step = 1
    while step < count:
        parts = [held]
        for multiple in range(1, 4):
            if step * multiple < count:
                ring = [(i, (i + step * multiple) % count) for i in range(count)]
                parts.append(lax.ppermute(held, "gx", ring))
        held = jnp.concatenate(parts, axis=0)
        if step == 1:
            held, tracer_received = lax.optimization_barrier((held, tracer_received))
        step *= 4
    reverse = held[::-1]
    doubled = jnp.concatenate([reverse, reverse], axis=0)
    packed_all = lax.dynamic_slice_in_dim(doubled, count - 1 - position, count, 0)
    left_value, right_value = interface_solve(packed_all, position, first_row.shape[0])
    wind_fields = (
        local_solve
        - left_spike[None, :, :, None] * left_value[:, :, None, :]
        - right_spike[None, :, :, None] * right_value[:, :, None, :]
    )
    tracer_windows = assemble_windows(
        tracer_main, tracer_halo, *tracer_received, offsets, position, block_count
    )
    tracers = advect_group(tracer_windows, shift_x, shift_y, field_count - 2)
    return (wind_fields, tracers)


def solution(mesh):
    return jax.shard_map(
        local,
        mesh=mesh,
        in_specs=(
            P(None, None, "gx", "gy"),
            P(None, "gx", "gy"),
            P(None, "gx", "gy"),
            P(None, "gy"),
            P(None, "gx", None),
            P(None, "gx"),
            P(None, "gx"),
        ),
        out_specs=(P(None, None, "gx", "gy"), P(None, None, "gx", "gy")),
        check_vma=False,
    )
```

```python
import jax
import jax.numpy as jnp
from jax import lax
from jax.sharding import PartitionSpec as P
from jax.experimental import pallas as pl
from jax.experimental.pallas import tpu as pltpu

BX = 16


PRECISE = lax.Precision.HIGHEST


def padded_2(block, sides, width):
    for axis, dim in sides:
        count = lax.axis_size(axis)
        forward = [(i, i + 1) for i in range(count - 1)]
        backward = [(target, source) for source, target in forward]
        low = lax.ppermute(
            lax.slice_in_dim(block, block.shape[dim] - width, None, axis=dim), axis, forward
        )
        high = lax.ppermute(lax.slice_in_dim(block, 0, width, axis=dim), axis, backward)
        block = jnp.concatenate([low, block, high], axis=dim)
    return block


def shifted_2(value, axis, steps):
    count = lax.axis_size(axis)
    leading, last = (max(0, -steps), min(count, count - steps))
    return lax.ppermute(value, axis, [(source, source + steps) for source in range(leading, last)])


def lagrange(displace):
    position = -displace
    weights = []
    for target in range(-2, 3):
        factor = jnp.ones_like(position)
        for anchor in range(-2, 3):
            if anchor != target:
                factor = factor * ((position - anchor) / (target - anchor))
        weights.append(factor)
    return weights


def interpolate(window, across, along, span_x, span_y):
    weights_x = lagrange(across)
    weights_y = lagrange(along)
    running_total = None
    for column_tap in range(5):
        partial_sum = weights_y[0] * window[..., column_tap : column_tap + span_x, 0:span_y]
        for row_tap in range(1, 5):
            partial_sum = (
                partial_sum
                + weights_y[row_tap]
                * window[..., column_tap : column_tap + span_x, row_tap : row_tap + span_y]
            )
        tap_term = weights_x[column_tap] * partial_sum
        running_total = tap_term if running_total is None else running_total + tap_term
    return running_total


def _solve_body(pos_ref, packed_ref, left_ref, right_ref, alpha_s, beta_s, p_s, q_s, f_s):
    count = packed_ref.shape[0]
    width = left_ref.shape[0]
    levels, lanes = left_ref.shape[1], left_ref.shape[2]
    p = jnp.zeros((width, levels, lanes), jnp.float32)
    q = jnp.zeros((levels, lanes), jnp.float32)
    for j in range(count):
        first = packed_ref[j, 0:width]
        last = packed_ref[j, width : 2 * width]
        coef = packed_ref[j, 2 * width]
        lead_left = jnp.broadcast_to(coef[:, 0:1], (levels, lanes))
        tail_left = jnp.broadcast_to(coef[:, 1:2], (levels, lanes))
        lead_right = jnp.broadcast_to(coef[:, 2:3], (levels, lanes))
        tail_right = jnp.broadcast_to(coef[:, 3:4], (levels, lanes))
        pivot = 1.0 + lead_left * q
        alpha = (first - lead_left * p) / pivot
        beta = -lead_right / pivot
        p_s[j] = p
        q_s[j] = q
        alpha_s[j] = alpha
        beta_s[j] = beta
        p = last - tail_left * p - tail_left * q * alpha
        q = -(tail_left * q * beta) - tail_right
    ahead = jnp.zeros((width, levels, lanes), jnp.float32)
    f_s[count] = ahead
    for j in range(count - 1, -1, -1):
        ahead = alpha_s[j] + beta_s[j] * ahead
        f_s[j] = ahead
    pos = pos_ref[0]
    left_ref[...] = p_s[pos] + q_s[pos] * f_s[pos]
    right_ref[...] = f_s[pos + 1]

def interface_solve(packed_all, position, width):
    count, _, levels, lanes = packed_all.shape
    out = jax.ShapeDtypeStruct((width, levels, lanes), jnp.float32)
    vmem = pltpu.VMEM
    return pl.pallas_call(
        _solve_body,
        out_shape=(out, out),
        in_specs=[pl.BlockSpec(memory_space=pltpu.SMEM), pl.BlockSpec(memory_space=vmem)],
        out_specs=(pl.BlockSpec(memory_space=vmem), pl.BlockSpec(memory_space=vmem)),
        scratch_shapes=[
            pltpu.VMEM((count, width, levels, lanes), jnp.float32),
            pltpu.VMEM((count, levels, lanes), jnp.float32),
            pltpu.VMEM((count, width, levels, lanes), jnp.float32),
            pltpu.VMEM((count, levels, lanes), jnp.float32),
            pltpu.VMEM((count + 1, width, levels, lanes), jnp.float32),
        ],
    )(jnp.reshape(position, (1,)).astype(jnp.int32), packed_all)


def halo_x(block, axis, width):
    count = lax.axis_size(axis)
    forward = [(i, i + 1) for i in range(count - 1)]
    backward = [(target, source) for source, target in forward]
    low = lax.ppermute(block[:, block.shape[1] - width :], axis, forward)
    high = lax.ppermute(block[:, 0:width], axis, backward)
    return jnp.concatenate([low, block, high], axis=1)


def halo_y(block, axis, width):
    count = lax.axis_size(axis)
    forward = [(i, i + 1) for i in range(count - 1)]
    backward = [(target, source) for source, target in forward]
    low = lax.ppermute(block[:, :, block.shape[2] - width :], axis, forward)
    high = lax.ppermute(block[:, :, 0:width], axis, backward)
    return jnp.concatenate([low, high], axis=2)


def source_of(offsets, run, block_count):
    blocks = run * block_count + jnp.arange(block_count, dtype=jnp.int32)
    return blocks - lax.dynamic_slice_in_dim(offsets, run * block_count, block_count)


def slot_rank(mask):
    return jnp.cumsum(mask.astype(jnp.int32)) - 1


def send_windows(main, halo, offsets, position, count, block_count):
    window = BX + 4
    cap = 4
    channels, _, rows_here = main.shape
    deltas = (-2, -1, 1, 2)
    received_main = {}
    received_halo = {}
    for delta in deltas:
        target = jnp.clip(position - delta, 0, count - 1)
        source = source_of(offsets, target, block_count)
        local_start = (source - position * block_count) * BX
        mask = (source >= position * block_count) & (source < (position + 1) * block_count)
        rank = slot_rank(mask)
        starts = [
            jnp.sum(jnp.where(mask & (rank == slot), local_start, 0)) for slot in range(cap)
        ]
        send_main = jnp.concatenate(
            [lax.dynamic_slice_in_dim(main, start, window, 1) for start in starts], axis=1
        )
        send_halo = jnp.concatenate(
            [lax.dynamic_slice_in_dim(halo, start, window, 2) for start in starts], axis=2
        )
        span = cap * window
        send_halo = jnp.pad(send_halo, ((0, 0), (0, 0), (0, rows_here - span)))
        sent = shifted_2(jnp.concatenate([send_main, send_halo], axis=1), "gx", -delta)
        received_main[delta] = sent[:, 0:span]
        received_halo[delta] = sent[:, span:, 0:span]
    return received_main, received_halo


def assemble_windows(main, halo, received_main, received_halo, offsets, position, block_count):
    window = BX + 4
    order = (-2, -1, 0, 1, 2)
    pieces_main = [main if delta == 0 else received_main[delta] for delta in order]
    pieces_halo = [halo if delta == 0 else received_halo[delta] for delta in order]
    bases = {}
    base = 0
    for delta, piece in zip(order, pieces_main):
        bases[delta] = base
        base += piece.shape[1]
    all_main = jnp.concatenate(pieces_main, axis=1)
    all_halo = jnp.concatenate(pieces_halo, axis=2)
    own_source = source_of(offsets, position, block_count)
    own_delta = own_source // block_count - position
    start_here = jnp.zeros((block_count,), jnp.int32)
    for delta in order:
        if delta == 0:
            candidate = bases[0] + (own_source - position * block_count) * BX
        else:
            rank = slot_rank(own_delta == delta)
            candidate = bases[delta] + rank * window
        start_here = jnp.where(own_delta == delta, candidate, start_here)
    window_main = jnp.stack(
        [lax.dynamic_slice_in_dim(all_main, start_here[b], window, 1) for b in range(block_count)]
    )
    window_halo = jnp.stack(
        [lax.dynamic_slice_in_dim(all_halo, start_here[b], window, 2) for b in range(block_count)]
    ).transpose(0, 1, 3, 2)
    return jnp.concatenate(
        [window_halo[..., 0:2], window_main, window_halo[..., 2:4]], axis=3
    )


def advect_group(windows, shift_x, shift_y, field_count):
    block_count = windows.shape[0]
    level_count, columns, rows_here = shift_x.shape
    windows = windows.reshape(block_count, field_count, level_count, BX + 4, rows_here + 4)
    across = shift_x.reshape(level_count, block_count, BX, rows_here).transpose(1, 0, 2, 3)[:, None]
    along = shift_y.reshape(level_count, block_count, BX, rows_here).transpose(1, 0, 2, 3)[:, None]
    interpolated = interpolate(windows, across, along, BX, rows_here)
    return interpolated.transpose(1, 2, 0, 3, 4).reshape(
        field_count, level_count, columns, rows_here
    )


def local(fields, shift_x, shift_y, block_offset, group_inverse, lower_coupling, upper_coupling):
    field_count, level_count, columns, rows_here = fields.shape
    block_count = columns // BX
    channels = field_count * level_count
    wind_channels = 2 * level_count
    count = lax.axis_size("gx")
    position = lax.axis_index("gx")
    padded = padded_2(fields, (("gx", 2), ("gy", 3)), 2).reshape(
        channels, columns + 4, rows_here + 4
    )
    main = padded[:, :, 2 : rows_here + 2]
    halo = jnp.concatenate(
        [padded[:, :, 0:2], padded[:, :, rows_here + 2 :]], axis=2
    ).transpose(0, 2, 1)
    offsets = block_offset[:, 0]
    wind_main, wind_halo = main[:wind_channels], halo[:wind_channels]
    tracer_main, tracer_halo = main[wind_channels:], halo[wind_channels:]
    wind_received = send_windows(wind_main, wind_halo, offsets, position, count, block_count)
    tracer_received = send_windows(tracer_main, tracer_halo, offsets, position, count, block_count)
    wind_windows = assemble_windows(
        wind_main, wind_halo, *wind_received, offsets, position, block_count
    )
    winds = advect_group(wind_windows, shift_x, shift_y, 2)
    local_solve = jnp.einsum("lij,wljy->wliy", group_inverse, winds, precision=PRECISE)
    lower_here = lower_coupling[:, 0]
    upper_here = upper_coupling[:, 0]
    left_spike = group_inverse[:, :, 0] * lower_here[:, None]
    right_spike = group_inverse[:, :, columns - 1] * upper_here[:, None]
    coef = jnp.stack(
        [left_spike[:, 0], left_spike[:, columns - 1], right_spike[:, 0], right_spike[:, columns - 1]],
        axis=-1,
    )
    coef_rows = jnp.pad(coef, ((0, 0), (0, rows_here - 4)))
    first_row = local_solve[:, :, 0, :]
    last_row = local_solve[:, :, columns - 1, :]
    packed = jnp.concatenate([first_row, last_row, coef_rows[None]], axis=0)
    held = packed[None]
    step = 1
    while step < count:
        ring = [(i, (i + step) % count) for i in range(count)]
        held = jnp.concatenate([held, lax.ppermute(held, "gx", ring)], axis=0)
        if step == 1:
            held, tracer_received = lax.optimization_barrier((held, tracer_received))
        step *= 2
    reverse = held[::-1]
    doubled = jnp.concatenate([reverse, reverse], axis=0)
    packed_all = lax.dynamic_slice_in_dim(doubled, count - 1 - position, count, 0)
    left_value, right_value = interface_solve(packed_all, position, first_row.shape[0])
    wind_fields = (
        local_solve
        - left_spike[None, :, :, None] * left_value[:, :, None, :]
        - right_spike[None, :, :, None] * right_value[:, :, None, :]
    )
    tracer_windows = assemble_windows(
        tracer_main, tracer_halo, *tracer_received, offsets, position, block_count
    )
    tracers = advect_group(tracer_windows, shift_x, shift_y, field_count - 2)
    return (wind_fields, tracers)


def solution(mesh):
    return jax.shard_map(
        local,
        mesh=mesh,
        in_specs=(
            P(None, None, "gx", "gy"),
            P(None, "gx", "gy"),
            P(None, "gx", "gy"),
            P(None, "gy"),
            P(None, "gx", None),
            P(None, "gx"),
            P(None, "gx"),
        ),
        out_specs=(P(None, None, "gx", "gy"), P(None, None, "gx", "gy")),
        check_vma=False,
    )
```

```python
import jax
import jax.numpy as jnp
from jax import lax
from jax.sharding import PartitionSpec as P
from jax.experimental import pallas as pl
from jax.experimental.pallas import tpu as pltpu

BX = 16


PRECISE = lax.Precision.HIGHEST


def padded_2(block, sides, width):
    for axis, dim in sides:
        count = lax.axis_size(axis)
        forward = [(i, i + 1) for i in range(count - 1)]
        backward = [(target, source) for source, target in forward]
        low = lax.ppermute(
            lax.slice_in_dim(block, block.shape[dim] - width, None, axis=dim), axis, forward
        )
        high = lax.ppermute(lax.slice_in_dim(block, 0, width, axis=dim), axis, backward)
        block = jnp.concatenate([low, block, high], axis=dim)
    return block


def shifted_2(value, axis, steps):
    count = lax.axis_size(axis)
    leading, last = (max(0, -steps), min(count, count - steps))
    return lax.ppermute(value, axis, [(source, source + steps) for source in range(leading, last)])


def lagrange(displace):
    position = -displace
    weights = []
    for target in range(-2, 3):
        factor = jnp.ones_like(position)
        for anchor in range(-2, 3):
            if anchor != target:
                factor = factor * ((position - anchor) / (target - anchor))
        weights.append(factor)
    return weights


def interpolate(window, across, along, span_x, span_y):
    weights_x = lagrange(across)
    weights_y = lagrange(along)
    running_total = None
    for column_tap in range(5):
        partial_sum = weights_y[0] * window[..., column_tap : column_tap + span_x, 0:span_y]
        for row_tap in range(1, 5):
            partial_sum = (
                partial_sum
                + weights_y[row_tap]
                * window[..., column_tap : column_tap + span_x, row_tap : row_tap + span_y]
            )
        tap_term = weights_x[column_tap] * partial_sum
        running_total = tap_term if running_total is None else running_total + tap_term
    return running_total


def _solve_body(pos_ref, packed_ref, left_ref, right_ref, alpha_s, beta_s, p_s, q_s, f_s):
    count = packed_ref.shape[0]
    width = left_ref.shape[0]
    levels, lanes = left_ref.shape[1], left_ref.shape[2]
    p = jnp.zeros((width, levels, lanes), jnp.float32)
    q = jnp.zeros((levels, lanes), jnp.float32)
    for j in range(count):
        first = packed_ref[j, 0:width]
        last = packed_ref[j, width : 2 * width]
        coef = packed_ref[j, 2 * width]
        lead_left = jnp.broadcast_to(coef[:, 0:1], (levels, lanes))
        tail_left = jnp.broadcast_to(coef[:, 1:2], (levels, lanes))
        lead_right = jnp.broadcast_to(coef[:, 2:3], (levels, lanes))
        tail_right = jnp.broadcast_to(coef[:, 3:4], (levels, lanes))
        pivot = 1.0 + lead_left * q
        alpha = (first - lead_left * p) / pivot
        beta = -lead_right / pivot
        p_s[j] = p
        q_s[j] = q
        alpha_s[j] = alpha
        beta_s[j] = beta
        p = last - tail_left * p - tail_left * q * alpha
        q = -(tail_left * q * beta) - tail_right
    ahead = jnp.zeros((width, levels, lanes), jnp.float32)
    f_s[count] = ahead
    for j in range(count - 1, -1, -1):
        ahead = alpha_s[j] + beta_s[j] * ahead
        f_s[j] = ahead
    pos = pos_ref[0]
    left_ref[...] = p_s[pos] + q_s[pos] * f_s[pos]
    right_ref[...] = f_s[pos + 1]

def interface_solve(packed_all, position, width):
    count, _, levels, lanes = packed_all.shape
    out = jax.ShapeDtypeStruct((width, levels, lanes), jnp.float32)
    vmem = pltpu.VMEM
    return pl.pallas_call(
        _solve_body,
        out_shape=(out, out),
        in_specs=[pl.BlockSpec(memory_space=pltpu.SMEM), pl.BlockSpec(memory_space=vmem)],
        out_specs=(pl.BlockSpec(memory_space=vmem), pl.BlockSpec(memory_space=vmem)),
        scratch_shapes=[
            pltpu.VMEM((count, width, levels, lanes), jnp.float32),
            pltpu.VMEM((count, levels, lanes), jnp.float32),
            pltpu.VMEM((count, width, levels, lanes), jnp.float32),
            pltpu.VMEM((count, levels, lanes), jnp.float32),
            pltpu.VMEM((count + 1, width, levels, lanes), jnp.float32),
        ],
    )(jnp.reshape(position, (1,)).astype(jnp.int32), packed_all)


def halos_at_once(block, width):
    count_x = lax.axis_size("gx")
    count_y = lax.axis_size("gy")
    columns, rows = block.shape[1], block.shape[2]

    def moved(piece, step_x, step_y):
        pairs = []
        for sx in range(count_x):
            for sy in range(count_y):
                tx, ty = sx + step_x, sy + step_y
                if 0 <= tx < count_x and 0 <= ty < count_y:
                    pairs.append((sx * count_y + sy, tx * count_y + ty))
        return lax.ppermute(piece, ("gx", "gy"), pairs)

    low_x = block[:, columns - width :]
    high_x = block[:, 0:width]
    left = moved(low_x, 1, 0)
    right = moved(high_x, -1, 0)
    below = moved(block[:, :, rows - width :], 0, 1)
    above = moved(block[:, :, 0:width], 0, -1)
    corner_ll = moved(low_x[:, :, rows - width :], 1, 1)
    corner_lh = moved(low_x[:, :, 0:width], 1, -1)
    corner_hl = moved(high_x[:, :, rows - width :], -1, 1)
    corner_hh = moved(high_x[:, :, 0:width], -1, -1)
    main = jnp.concatenate([left, block, right], axis=1)
    low_rows = jnp.concatenate([corner_ll, below, corner_hl], axis=1)
    high_rows = jnp.concatenate([corner_lh, above, corner_hh], axis=1)
    halo = jnp.concatenate([low_rows, high_rows], axis=2).transpose(0, 2, 1)
    return main, halo


def halo_x(block, axis, width):
    count = lax.axis_size(axis)
    forward = [(i, i + 1) for i in range(count - 1)]
    backward = [(target, source) for source, target in forward]
    low = lax.ppermute(block[:, block.shape[1] - width :], axis, forward)
    high = lax.ppermute(block[:, 0:width], axis, backward)
    return jnp.concatenate([low, block, high], axis=1)


def halo_y(block, axis, width):
    count = lax.axis_size(axis)
    forward = [(i, i + 1) for i in range(count - 1)]
    backward = [(target, source) for source, target in forward]
    low = lax.ppermute(block[:, :, block.shape[2] - width :], axis, forward)
    high = lax.ppermute(block[:, :, 0:width], axis, backward)
    return jnp.concatenate([low, high], axis=2)


def source_of(offsets, run, block_count):
    blocks = run * block_count + jnp.arange(block_count, dtype=jnp.int32)
    return blocks - lax.dynamic_slice_in_dim(offsets, run * block_count, block_count)


def slot_rank(mask):
    return jnp.cumsum(mask.astype(jnp.int32)) - 1


def send_windows(main, halo, offsets, position, count, block_count):
    window = BX + 4
    cap = 4
    channels, _, rows_here = main.shape
    deltas = (-2, -1, 1, 2)
    received_main = {}
    received_halo = {}
    for delta in deltas:
        target = jnp.clip(position - delta, 0, count - 1)
        source = source_of(offsets, target, block_count)
        local_start = (source - position * block_count) * BX
        mask = (source >= position * block_count) & (source < (position + 1) * block_count)
        rank = slot_rank(mask)
        starts = [
            jnp.sum(jnp.where(mask & (rank == slot), local_start, 0)) for slot in range(cap)
        ]
        send_main = jnp.concatenate(
            [lax.dynamic_slice_in_dim(main, start, window, 1) for start in starts], axis=1
        )
        send_halo = jnp.concatenate(
            [lax.dynamic_slice_in_dim(halo, start, window, 2) for start in starts], axis=2
        )
        span = cap * window
        send_halo = jnp.pad(send_halo, ((0, 0), (0, 0), (0, rows_here - span)))
        sent = shifted_2(jnp.concatenate([send_main, send_halo], axis=1), "gx", -delta)
        received_main[delta] = sent[:, 0:span]
        received_halo[delta] = sent[:, span:, 0:span]
    return received_main, received_halo


def assemble_windows(main, halo, received_main, received_halo, offsets, position, block_count):
    window = BX + 4
    order = (-2, -1, 0, 1, 2)
    pieces_main = [main if delta == 0 else received_main[delta] for delta in order]
    pieces_halo = [halo if delta == 0 else received_halo[delta] for delta in order]
    bases = {}
    base = 0
    for delta, piece in zip(order, pieces_main):
        bases[delta] = base
        base += piece.shape[1]
    all_main = jnp.concatenate(pieces_main, axis=1)
    all_halo = jnp.concatenate(pieces_halo, axis=2)
    own_source = source_of(offsets, position, block_count)
    own_delta = own_source // block_count - position
    start_here = jnp.zeros((block_count,), jnp.int32)
    for delta in order:
        if delta == 0:
            candidate = bases[0] + (own_source - position * block_count) * BX
        else:
            rank = slot_rank(own_delta == delta)
            candidate = bases[delta] + rank * window
        start_here = jnp.where(own_delta == delta, candidate, start_here)
    window_main = jnp.stack(
        [lax.dynamic_slice_in_dim(all_main, start_here[b], window, 1) for b in range(block_count)]
    )
    window_halo = jnp.stack(
        [lax.dynamic_slice_in_dim(all_halo, start_here[b], window, 2) for b in range(block_count)]
    ).transpose(0, 1, 3, 2)
    return jnp.concatenate(
        [window_halo[..., 0:2], window_main, window_halo[..., 2:4]], axis=3
    )


def advect_group(windows, shift_x, shift_y, field_count):
    block_count = windows.shape[0]
    level_count, columns, rows_here = shift_x.shape
    windows = windows.reshape(block_count, field_count, level_count, BX + 4, rows_here + 4)
    across = shift_x.reshape(level_count, block_count, BX, rows_here).transpose(1, 0, 2, 3)[:, None]
    along = shift_y.reshape(level_count, block_count, BX, rows_here).transpose(1, 0, 2, 3)[:, None]
    interpolated = interpolate(windows, across, along, BX, rows_here)
    return interpolated.transpose(1, 2, 0, 3, 4).reshape(
        field_count, level_count, columns, rows_here
    )


def local(fields, shift_x, shift_y, block_offset, group_inverse, lower_coupling, upper_coupling):
    field_count, level_count, columns, rows_here = fields.shape
    block_count = columns // BX
    channels = field_count * level_count
    wind_channels = 2 * level_count
    count = lax.axis_size("gx")
    position = lax.axis_index("gx")
    flat = fields.reshape(channels, columns, rows_here)
    main, halo = halos_at_once(flat, 2)
    offsets = block_offset[:, 0]
    wind_main, wind_halo = main[:wind_channels], halo[:wind_channels]
    tracer_main, tracer_halo = main[wind_channels:], halo[wind_channels:]
    wind_received = send_windows(wind_main, wind_halo, offsets, position, count, block_count)
    tracer_received = send_windows(tracer_main, tracer_halo, offsets, position, count, block_count)
    wind_windows = assemble_windows(
        wind_main, wind_halo, *wind_received, offsets, position, block_count
    )
    winds = advect_group(wind_windows, shift_x, shift_y, 2)
    local_solve = jnp.einsum("lij,wljy->wliy", group_inverse, winds, precision=PRECISE)
    lower_here = lower_coupling[:, 0]
    upper_here = upper_coupling[:, 0]
    left_spike = group_inverse[:, :, 0] * lower_here[:, None]
    right_spike = group_inverse[:, :, columns - 1] * upper_here[:, None]
    coef = jnp.stack(
        [left_spike[:, 0], left_spike[:, columns - 1], right_spike[:, 0], right_spike[:, columns - 1]],
        axis=-1,
    )
    coef_rows = jnp.pad(coef, ((0, 0), (0, rows_here - 4)))
    first_row = local_solve[:, :, 0, :]
    last_row = local_solve[:, :, columns - 1, :]
    packed = jnp.concatenate([first_row, last_row, coef_rows[None]], axis=0)
    held = packed[None]
    step = 1
    while step < count:
        ring = [(i, (i + step) % count) for i in range(count)]
        held = jnp.concatenate([held, lax.ppermute(held, "gx", ring)], axis=0)
        if step == 1:
            held, tracer_received = lax.optimization_barrier((held, tracer_received))
        step *= 2
    reverse = held[::-1]
    doubled = jnp.concatenate([reverse, reverse], axis=0)
    packed_all = lax.dynamic_slice_in_dim(doubled, count - 1 - position, count, 0)
    left_value, right_value = interface_solve(packed_all, position, first_row.shape[0])
    wind_fields = (
        local_solve
        - left_spike[None, :, :, None] * left_value[:, :, None, :]
        - right_spike[None, :, :, None] * right_value[:, :, None, :]
    )
    tracer_windows = assemble_windows(
        tracer_main, tracer_halo, *tracer_received, offsets, position, block_count
    )
    tracers = advect_group(tracer_windows, shift_x, shift_y, field_count - 2)
    return (wind_fields, tracers)


def solution(mesh):
    return jax.shard_map(
        local,
        mesh=mesh,
        in_specs=(
            P(None, None, "gx", "gy"),
            P(None, "gx", "gy"),
            P(None, "gx", "gy"),
            P(None, "gy"),
            P(None, "gx", None),
            P(None, "gx"),
            P(None, "gx"),
        ),
        out_specs=(P(None, None, "gx", "gy"), P(None, None, "gx", "gy")),
        check_vma=False,
    )
```

```python
import jax
import jax.numpy as jnp
from jax import lax
from jax.sharding import PartitionSpec as P
from jax.experimental import pallas as pl
from jax.experimental.pallas import tpu as pltpu

BX = 16


PRECISE = lax.Precision.HIGHEST


def padded_2(block, sides, width):
    for axis, dim in sides:
        count = lax.axis_size(axis)
        forward = [(i, i + 1) for i in range(count - 1)]
        backward = [(target, source) for source, target in forward]
        low = lax.ppermute(
            lax.slice_in_dim(block, block.shape[dim] - width, None, axis=dim), axis, forward
        )
        high = lax.ppermute(lax.slice_in_dim(block, 0, width, axis=dim), axis, backward)
        block = jnp.concatenate([low, block, high], axis=dim)
    return block


def shifted_2(value, axis, steps):
    count = lax.axis_size(axis)
    leading, last = (max(0, -steps), min(count, count - steps))
    return lax.ppermute(value, axis, [(source, source + steps) for source in range(leading, last)])


def lagrange(displace):
    position = -displace
    weights = []
    for target in range(-2, 3):
        factor = jnp.ones_like(position)
        for anchor in range(-2, 3):
            if anchor != target:
                factor = factor * ((position - anchor) / (target - anchor))
        weights.append(factor)
    return weights


def interpolate(window, across, along, span_x, span_y):
    weights_x = lagrange(across)
    weights_y = lagrange(along)
    running_total = None
    for column_tap in range(5):
        partial_sum = weights_y[0] * window[..., column_tap : column_tap + span_x, 0:span_y]
        for row_tap in range(1, 5):
            partial_sum = (
                partial_sum
                + weights_y[row_tap]
                * window[..., column_tap : column_tap + span_x, row_tap : row_tap + span_y]
            )
        tap_term = weights_x[column_tap] * partial_sum
        running_total = tap_term if running_total is None else running_total + tap_term
    return running_total


def _solve_body(pos_ref, packed_ref, left_ref, right_ref, alpha_s, beta_s, p_s, q_s, f_s):
    count = packed_ref.shape[0]
    width = left_ref.shape[0]
    levels, lanes = left_ref.shape[1], left_ref.shape[2]
    p = jnp.zeros((width, levels, lanes), jnp.float32)
    q = jnp.zeros((levels, lanes), jnp.float32)
    for j in range(count):
        first = packed_ref[j, 0:width]
        last = packed_ref[j, width : 2 * width]
        coef = packed_ref[j, 2 * width]
        lead_left = jnp.broadcast_to(coef[:, 0:1], (levels, lanes))
        tail_left = jnp.broadcast_to(coef[:, 1:2], (levels, lanes))
        lead_right = jnp.broadcast_to(coef[:, 2:3], (levels, lanes))
        tail_right = jnp.broadcast_to(coef[:, 3:4], (levels, lanes))
        pivot = 1.0 + lead_left * q
        alpha = (first - lead_left * p) / pivot
        beta = -lead_right / pivot
        p_s[j] = p
        q_s[j] = q
        alpha_s[j] = alpha
        beta_s[j] = beta
        p = last - tail_left * p - tail_left * q * alpha
        q = -(tail_left * q * beta) - tail_right
    ahead = jnp.zeros((width, levels, lanes), jnp.float32)
    f_s[count] = ahead
    for j in range(count - 1, -1, -1):
        ahead = alpha_s[j] + beta_s[j] * ahead
        f_s[j] = ahead
    pos = pos_ref[0]
    left_ref[...] = p_s[pos] + q_s[pos] * f_s[pos]
    right_ref[...] = f_s[pos + 1]

def interface_solve(packed_all, position, width):
    count, _, levels, lanes = packed_all.shape
    out = jax.ShapeDtypeStruct((width, levels, lanes), jnp.float32)
    vmem = pltpu.VMEM
    return pl.pallas_call(
        _solve_body,
        out_shape=(out, out),
        in_specs=[pl.BlockSpec(memory_space=pltpu.SMEM), pl.BlockSpec(memory_space=vmem)],
        out_specs=(pl.BlockSpec(memory_space=vmem), pl.BlockSpec(memory_space=vmem)),
        scratch_shapes=[
            pltpu.VMEM((count, width, levels, lanes), jnp.float32),
            pltpu.VMEM((count, levels, lanes), jnp.float32),
            pltpu.VMEM((count, width, levels, lanes), jnp.float32),
            pltpu.VMEM((count, levels, lanes), jnp.float32),
            pltpu.VMEM((count + 1, width, levels, lanes), jnp.float32),
        ],
    )(jnp.reshape(position, (1,)).astype(jnp.int32), packed_all)


def halo_x(block, axis, width):
    count = lax.axis_size(axis)
    forward = [(i, i + 1) for i in range(count - 1)]
    backward = [(target, source) for source, target in forward]
    low = lax.ppermute(block[:, block.shape[1] - width :], axis, forward)
    high = lax.ppermute(block[:, 0:width], axis, backward)
    return jnp.concatenate([low, block, high], axis=1)


def halo_y(block, axis, width):
    count = lax.axis_size(axis)
    forward = [(i, i + 1) for i in range(count - 1)]
    backward = [(target, source) for source, target in forward]
    low = lax.ppermute(block[:, :, block.shape[2] - width :], axis, forward)
    high = lax.ppermute(block[:, :, 0:width], axis, backward)
    return jnp.concatenate([low, high], axis=2)


def source_of(offsets, run, block_count):
    blocks = run * block_count + jnp.arange(block_count, dtype=jnp.int32)
    return blocks - lax.dynamic_slice_in_dim(offsets, run * block_count, block_count)


def slot_rank(mask):
    return jnp.cumsum(mask.astype(jnp.int32)) - 1


def send_windows(main, halo, offsets, position, count, block_count):
    window = BX + 4
    cap = 4
    channels, _, rows_here = main.shape
    deltas = (-2, -1, 1, 2)
    received_main = {}
    received_halo = {}
    for delta in deltas:
        target = jnp.clip(position - delta, 0, count - 1)
        source = source_of(offsets, target, block_count)
        local_start = (source - position * block_count) * BX
        mask = (source >= position * block_count) & (source < (position + 1) * block_count)
        rank = slot_rank(mask)
        starts = [
            jnp.sum(jnp.where(mask & (rank == slot), local_start, 0)) for slot in range(cap)
        ]
        send_main = jnp.concatenate(
            [lax.dynamic_slice_in_dim(main, start, window, 1) for start in starts], axis=1
        )
        send_halo = jnp.concatenate(
            [lax.dynamic_slice_in_dim(halo, start, window, 2) for start in starts], axis=2
        )
        span = cap * window
        send_halo = jnp.pad(send_halo, ((0, 0), (0, 0), (0, rows_here - span)))
        sent = shifted_2(jnp.concatenate([send_main, send_halo], axis=1), "gx", -delta)
        received_main[delta] = sent[:, 0:span]
        received_halo[delta] = sent[:, span:, 0:span]
    return received_main, received_halo


def assemble_windows(main, halo, received_main, received_halo, offsets, position, block_count):
    window = BX + 4
    order = (-2, -1, 0, 1, 2)
    pieces_main = [main if delta == 0 else received_main[delta] for delta in order]
    pieces_halo = [halo if delta == 0 else received_halo[delta] for delta in order]
    bases = {}
    base = 0
    for delta, piece in zip(order, pieces_main):
        bases[delta] = base
        base += piece.shape[1]
    all_main = jnp.concatenate(pieces_main, axis=1)
    all_halo = jnp.concatenate(pieces_halo, axis=2)
    own_source = source_of(offsets, position, block_count)
    own_delta = own_source // block_count - position
    start_here = jnp.zeros((block_count,), jnp.int32)
    for delta in order:
        if delta == 0:
            candidate = bases[0] + (own_source - position * block_count) * BX
        else:
            rank = slot_rank(own_delta == delta)
            candidate = bases[delta] + rank * window
        start_here = jnp.where(own_delta == delta, candidate, start_here)
    window_main = jnp.stack(
        [lax.dynamic_slice_in_dim(all_main, start_here[b], window, 1) for b in range(block_count)]
    )
    window_halo = jnp.stack(
        [lax.dynamic_slice_in_dim(all_halo, start_here[b], window, 2) for b in range(block_count)]
    ).transpose(0, 1, 3, 2)
    return jnp.concatenate(
        [window_halo[..., 0:2], window_main, window_halo[..., 2:4]], axis=3
    )


def advect_group(windows, shift_x, shift_y, field_count):
    block_count = windows.shape[0]
    level_count, columns, rows_here = shift_x.shape
    windows = windows.reshape(block_count, field_count, level_count, BX + 4, rows_here + 4)
    across = shift_x.reshape(level_count, block_count, BX, rows_here).transpose(1, 0, 2, 3)[:, None]
    along = shift_y.reshape(level_count, block_count, BX, rows_here).transpose(1, 0, 2, 3)[:, None]
    interpolated = interpolate(windows, across, along, BX, rows_here)
    return interpolated.transpose(1, 2, 0, 3, 4).reshape(
        field_count, level_count, columns, rows_here
    )


def local(fields, shift_x, shift_y, block_offset, group_inverse, lower_coupling, upper_coupling):
    field_count, level_count, columns, rows_here = fields.shape
    block_count = columns // BX
    channels = field_count * level_count
    wind_channels = 2 * level_count
    count = lax.axis_size("gx")
    position = lax.axis_index("gx")
    flat = fields.reshape(channels, columns, rows_here)
    main = halo_x(flat, "gx", 2)
    halo = halo_y(main, "gy", 2).transpose(0, 2, 1)
    offsets = block_offset[:, 0]
    wind_main, wind_halo = main[:wind_channels], halo[:wind_channels]
    tracer_main, tracer_halo = main[wind_channels:], halo[wind_channels:]
    wind_received = send_windows(wind_main, wind_halo, offsets, position, count, block_count)
    tracer_received = send_windows(tracer_main, tracer_halo, offsets, position, count, block_count)
    wind_windows = assemble_windows(
        wind_main, wind_halo, *wind_received, offsets, position, block_count
    )
    winds = advect_group(wind_windows, shift_x, shift_y, 2)
    local_solve = jnp.einsum("lij,wljy->wliy", group_inverse, winds, precision=PRECISE)
    lower_here = lower_coupling[:, 0]
    upper_here = upper_coupling[:, 0]
    left_spike = group_inverse[:, :, 0] * lower_here[:, None]
    right_spike = group_inverse[:, :, columns - 1] * upper_here[:, None]
    coef = jnp.stack(
        [left_spike[:, 0], left_spike[:, columns - 1], right_spike[:, 0], right_spike[:, columns - 1]],
        axis=-1,
    )
    coef_rows = jnp.pad(coef, ((0, 0), (0, rows_here - 4)))
    first_row = local_solve[:, :, 0, :]
    last_row = local_solve[:, :, columns - 1, :]
    packed = jnp.concatenate([first_row, last_row, coef_rows[None]], axis=0)
    slots = lax.dynamic_update_slice_in_dim(
        jnp.zeros((count,) + packed.shape, packed.dtype), packed[None], position, 0
    )
    packed_all = lax.psum(slots, "gx")
    tracer_received = lax.optimization_barrier((slots, tracer_received))[1]
    left_value, right_value = interface_solve(packed_all, position, first_row.shape[0])
    wind_fields = (
        local_solve
        - left_spike[None, :, :, None] * left_value[:, :, None, :]
        - right_spike[None, :, :, None] * right_value[:, :, None, :]
    )
    tracer_windows = assemble_windows(
        tracer_main, tracer_halo, *tracer_received, offsets, position, block_count
    )
    tracers = advect_group(tracer_windows, shift_x, shift_y, field_count - 2)
    return (wind_fields, tracers)


def solution(mesh):
    return jax.shard_map(
        local,
        mesh=mesh,
        in_specs=(
            P(None, None, "gx", "gy"),
            P(None, "gx", "gy"),
            P(None, "gx", "gy"),
            P(None, "gy"),
            P(None, "gx", None),
            P(None, "gx"),
            P(None, "gx"),
        ),
        out_specs=(P(None, None, "gx", "gy"), P(None, None, "gx", "gy")),
        check_vma=False,
    )
```

```python
import jax
import jax.numpy as jnp
from jax import lax
from jax.sharding import PartitionSpec as P
from jax.experimental import pallas as pl
from jax.experimental.pallas import tpu as pltpu

BX = 16


PRECISE = lax.Precision.HIGHEST


def padded_2(block, sides, width):
    for axis, dim in sides:
        count = lax.axis_size(axis)
        forward = [(i, i + 1) for i in range(count - 1)]
        backward = [(target, source) for source, target in forward]
        low = lax.ppermute(
            lax.slice_in_dim(block, block.shape[dim] - width, None, axis=dim), axis, forward
        )
        high = lax.ppermute(lax.slice_in_dim(block, 0, width, axis=dim), axis, backward)
        block = jnp.concatenate([low, block, high], axis=dim)
    return block


def shifted_2(value, axis, steps):
    count = lax.axis_size(axis)
    leading, last = (max(0, -steps), min(count, count - steps))
    return lax.ppermute(value, axis, [(source, source + steps) for source in range(leading, last)])


def lagrange(displace):
    position = -displace
    weights = []
    for target in range(-2, 3):
        factor = jnp.ones_like(position)
        for anchor in range(-2, 3):
            if anchor != target:
                factor = factor * ((position - anchor) / (target - anchor))
        weights.append(factor)
    return weights


def interpolate(window, across, along, span_x, span_y):
    weights_x = lagrange(across)
    weights_y = lagrange(along)
    running_total = None
    for column_tap in range(5):
        partial_sum = weights_y[0] * window[..., column_tap : column_tap + span_x, 0:span_y]
        for row_tap in range(1, 5):
            partial_sum = (
                partial_sum
                + weights_y[row_tap]
                * window[..., column_tap : column_tap + span_x, row_tap : row_tap + span_y]
            )
        tap_term = weights_x[column_tap] * partial_sum
        running_total = tap_term if running_total is None else running_total + tap_term
    return running_total


def _solve_body(pos_ref, packed_ref, left_ref, right_ref, alpha_s, beta_s, p_s, q_s, f_s):
    count = packed_ref.shape[0]
    width = left_ref.shape[0]
    levels, lanes = left_ref.shape[1], left_ref.shape[2]
    p = jnp.zeros((width, levels, lanes), jnp.float32)
    q = jnp.zeros((levels, lanes), jnp.float32)
    for j in range(count):
        first = packed_ref[j, 0:width]
        last = packed_ref[j, width : 2 * width]
        coef = packed_ref[j, 2 * width]
        lead_left = jnp.broadcast_to(coef[:, 0:1], (levels, lanes))
        tail_left = jnp.broadcast_to(coef[:, 1:2], (levels, lanes))
        lead_right = jnp.broadcast_to(coef[:, 2:3], (levels, lanes))
        tail_right = jnp.broadcast_to(coef[:, 3:4], (levels, lanes))
        pivot = 1.0 + lead_left * q
        alpha = (first - lead_left * p) / pivot
        beta = -lead_right / pivot
        p_s[j] = p
        q_s[j] = q
        alpha_s[j] = alpha
        beta_s[j] = beta
        p = last - tail_left * p - tail_left * q * alpha
        q = -(tail_left * q * beta) - tail_right
    ahead = jnp.zeros((width, levels, lanes), jnp.float32)
    f_s[count] = ahead
    for j in range(count - 1, -1, -1):
        ahead = alpha_s[j] + beta_s[j] * ahead
        f_s[j] = ahead
    pos = pos_ref[0]
    left_ref[...] = p_s[pos] + q_s[pos] * f_s[pos]
    right_ref[...] = f_s[pos + 1]

def interface_solve(packed_all, position, width):
    count, _, levels, lanes = packed_all.shape
    out = jax.ShapeDtypeStruct((width, levels, lanes), jnp.float32)
    vmem = pltpu.VMEM
    return pl.pallas_call(
        _solve_body,
        out_shape=(out, out),
        in_specs=[pl.BlockSpec(memory_space=pltpu.SMEM), pl.BlockSpec(memory_space=vmem)],
        out_specs=(pl.BlockSpec(memory_space=vmem), pl.BlockSpec(memory_space=vmem)),
        scratch_shapes=[
            pltpu.VMEM((count, width, levels, lanes), jnp.float32),
            pltpu.VMEM((count, levels, lanes), jnp.float32),
            pltpu.VMEM((count, width, levels, lanes), jnp.float32),
            pltpu.VMEM((count, levels, lanes), jnp.float32),
            pltpu.VMEM((count + 1, width, levels, lanes), jnp.float32),
        ],
    )(jnp.reshape(position, (1,)).astype(jnp.int32), packed_all)


def halo_x(block, axis, width):
    count = lax.axis_size(axis)
    forward = [(i, i + 1) for i in range(count - 1)]
    backward = [(target, source) for source, target in forward]
    low = lax.ppermute(block[:, block.shape[1] - width :], axis, forward)
    high = lax.ppermute(block[:, 0:width], axis, backward)
    return jnp.concatenate([low, block, high], axis=1)


def halo_y(block, axis, width):
    count = lax.axis_size(axis)
    forward = [(i, i + 1) for i in range(count - 1)]
    backward = [(target, source) for source, target in forward]
    low = lax.ppermute(block[:, :, block.shape[2] - width :], axis, forward)
    high = lax.ppermute(block[:, :, 0:width], axis, backward)
    return jnp.concatenate([low, high], axis=2)


def source_of(offsets, run, block_count):
    blocks = run * block_count + jnp.arange(block_count, dtype=jnp.int32)
    return blocks - lax.dynamic_slice_in_dim(offsets, run * block_count, block_count)


def slot_rank(mask):
    return jnp.cumsum(mask.astype(jnp.int32)) - 1


def send_windows(main, halo, offsets, position, count, block_count):
    window = BX + 4
    cap = 4
    channels, _, rows_here = main.shape
    deltas = (-2, -1, 1, 2)
    received_main = {}
    received_halo = {}
    for delta in deltas:
        target = jnp.clip(position - delta, 0, count - 1)
        source = source_of(offsets, target, block_count)
        local_start = (source - position * block_count) * BX
        mask = (source >= position * block_count) & (source < (position + 1) * block_count)
        rank = slot_rank(mask)
        starts = [
            jnp.sum(jnp.where(mask & (rank == slot), local_start, 0)) for slot in range(cap)
        ]
        send_main = jnp.concatenate(
            [lax.dynamic_slice_in_dim(main, start, window, 1) for start in starts], axis=1
        )
        send_halo = jnp.concatenate(
            [lax.dynamic_slice_in_dim(halo, start, window, 2) for start in starts], axis=2
        )
        span = cap * window
        send_halo = jnp.pad(send_halo, ((0, 0), (0, 0), (0, rows_here - span)))
        sent = shifted_2(jnp.concatenate([send_main, send_halo], axis=1), "gx", -delta)
        received_main[delta] = sent[:, 0:span]
        received_halo[delta] = sent[:, span:, 0:span]
    return received_main, received_halo


def assemble_windows(main, halo, received_main, received_halo, offsets, position, block_count):
    window = BX + 4
    order = (-2, -1, 0, 1, 2)
    pieces_main = [main if delta == 0 else received_main[delta] for delta in order]
    pieces_halo = [halo if delta == 0 else received_halo[delta] for delta in order]
    bases = {}
    base = 0
    for delta, piece in zip(order, pieces_main):
        bases[delta] = base
        base += piece.shape[1]
    all_main = jnp.concatenate(pieces_main, axis=1)
    all_halo = jnp.concatenate(pieces_halo, axis=2)
    own_source = source_of(offsets, position, block_count)
    own_delta = own_source // block_count - position
    start_here = jnp.zeros((block_count,), jnp.int32)
    for delta in order:
        if delta == 0:
            candidate = bases[0] + (own_source - position * block_count) * BX
        else:
            rank = slot_rank(own_delta == delta)
            candidate = bases[delta] + rank * window
        start_here = jnp.where(own_delta == delta, candidate, start_here)
    window_main = jnp.stack(
        [lax.dynamic_slice_in_dim(all_main, start_here[b], window, 1) for b in range(block_count)]
    )
    window_halo = jnp.stack(
        [lax.dynamic_slice_in_dim(all_halo, start_here[b], window, 2) for b in range(block_count)]
    ).transpose(0, 1, 3, 2)
    return jnp.concatenate(
        [window_halo[..., 0:2], window_main, window_halo[..., 2:4]], axis=3
    )


def advect_group(windows, across, along, field_count):
    block_count, _, level_count, _, rows_here = across.shape
    columns = block_count * BX
    windows = windows.reshape(block_count, field_count, level_count, BX + 4, rows_here + 4)
    interpolated = interpolate(windows, across, along, BX, rows_here)
    return interpolated.transpose(1, 2, 0, 3, 4).reshape(
        field_count, level_count, columns, rows_here
    )


def local(fields, shift_x, shift_y, block_offset, group_inverse, lower_coupling, upper_coupling):
    field_count, level_count, columns, rows_here = fields.shape
    block_count = columns // BX
    channels = field_count * level_count
    wind_channels = 2 * level_count
    count = lax.axis_size("gx")
    position = lax.axis_index("gx")
    flat = fields.reshape(channels, columns, rows_here)
    main = halo_x(flat, "gx", 2)
    halo = halo_y(main, "gy", 2).transpose(0, 2, 1)
    offsets = block_offset[:, 0]
    across = shift_x.reshape(level_count, block_count, BX, rows_here).transpose(1, 0, 2, 3)[:, None]
    along = shift_y.reshape(level_count, block_count, BX, rows_here).transpose(1, 0, 2, 3)[:, None]
    across, along, main, halo = lax.optimization_barrier((across, along, main, halo))
    wind_main, wind_halo = main[:wind_channels], halo[:wind_channels]
    tracer_main, tracer_halo = main[wind_channels:], halo[wind_channels:]
    wind_received = send_windows(wind_main, wind_halo, offsets, position, count, block_count)
    tracer_received = send_windows(tracer_main, tracer_halo, offsets, position, count, block_count)
    wind_windows = assemble_windows(
        wind_main, wind_halo, *wind_received, offsets, position, block_count
    )
    winds = advect_group(wind_windows, across, along, 2)
    local_solve = jnp.einsum("lij,wljy->wliy", group_inverse, winds, precision=PRECISE)
    lower_here = lower_coupling[:, 0]
    upper_here = upper_coupling[:, 0]
    left_spike = group_inverse[:, :, 0] * lower_here[:, None]
    right_spike = group_inverse[:, :, columns - 1] * upper_here[:, None]
    coef = jnp.stack(
        [left_spike[:, 0], left_spike[:, columns - 1], right_spike[:, 0], right_spike[:, columns - 1]],
        axis=-1,
    )
    coef_rows = jnp.pad(coef, ((0, 0), (0, rows_here - 4)))
    first_row = local_solve[:, :, 0, :]
    last_row = local_solve[:, :, columns - 1, :]
    packed = jnp.concatenate([first_row, last_row, coef_rows[None]], axis=0)
    held = packed[None]
    step = 1
    while step < count:
        ring = [(i, (i + step) % count) for i in range(count)]
        held = jnp.concatenate([held, lax.ppermute(held, "gx", ring)], axis=0)
        if step == 1:
            held, tracer_received = lax.optimization_barrier((held, tracer_received))
        step *= 2
    reverse = held[::-1]
    doubled = jnp.concatenate([reverse, reverse], axis=0)
    packed_all = lax.dynamic_slice_in_dim(doubled, count - 1 - position, count, 0)
    left_value, right_value = interface_solve(packed_all, position, first_row.shape[0])
    wind_fields = (
        local_solve
        - left_spike[None, :, :, None] * left_value[:, :, None, :]
        - right_spike[None, :, :, None] * right_value[:, :, None, :]
    )
    tracer_windows = assemble_windows(
        tracer_main, tracer_halo, *tracer_received, offsets, position, block_count
    )
    tracers = advect_group(tracer_windows, across, along, field_count - 2)
    return (wind_fields, tracers)


def solution(mesh):
    return jax.shard_map(
        local,
        mesh=mesh,
        in_specs=(
            P(None, None, "gx", "gy"),
            P(None, "gx", "gy"),
            P(None, "gx", "gy"),
            P(None, "gy"),
            P(None, "gx", None),
            P(None, "gx"),
            P(None, "gx"),
        ),
        out_specs=(P(None, None, "gx", "gy"), P(None, None, "gx", "gy")),
        check_vma=False,
    )
```

```python
import jax
import jax.numpy as jnp
from jax import lax
from jax.sharding import PartitionSpec as P
from jax.experimental import pallas as pl
from jax.experimental.pallas import tpu as pltpu

BX = 16


PRECISE = lax.Precision.HIGHEST


def padded_2(block, sides, width):
    for axis, dim in sides:
        count = lax.axis_size(axis)
        forward = [(i, i + 1) for i in range(count - 1)]
        backward = [(target, source) for source, target in forward]
        low = lax.ppermute(
            lax.slice_in_dim(block, block.shape[dim] - width, None, axis=dim), axis, forward
        )
        high = lax.ppermute(lax.slice_in_dim(block, 0, width, axis=dim), axis, backward)
        block = jnp.concatenate([low, block, high], axis=dim)
    return block


def shifted_2(value, axis, steps):
    count = lax.axis_size(axis)
    leading, last = (max(0, -steps), min(count, count - steps))
    return lax.ppermute(value, axis, [(source, source + steps) for source in range(leading, last)])


def lagrange(displace):
    position = -displace
    weights = []
    for target in range(-2, 3):
        factor = jnp.ones_like(position)
        for anchor in range(-2, 3):
            if anchor != target:
                factor = factor * ((position - anchor) / (target - anchor))
        weights.append(factor)
    return weights


def interpolate(window, across, along, span_x, span_y):
    weights_x = lagrange(across)
    weights_y = lagrange(along)
    running_total = None
    for column_tap in range(5):
        partial_sum = weights_y[0] * window[..., column_tap : column_tap + span_x, 0:span_y]
        for row_tap in range(1, 5):
            partial_sum = (
                partial_sum
                + weights_y[row_tap]
                * window[..., column_tap : column_tap + span_x, row_tap : row_tap + span_y]
            )
        tap_term = weights_x[column_tap] * partial_sum
        running_total = tap_term if running_total is None else running_total + tap_term
    return running_total


def _solve_body(pos_ref, packed_ref, solve_ref, lspike_ref, rspike_ref, out_ref, alpha_s, beta_s, p_s, q_s, f_s):
    count = packed_ref.shape[0]
    width, levels = out_ref.shape[0], out_ref.shape[1]
    lanes = out_ref.shape[3]
    p = jnp.zeros((width, levels, lanes), jnp.float32)
    q = jnp.zeros((levels, lanes), jnp.float32)
    for j in range(count):
        first = packed_ref[j, 0:width]
        last = packed_ref[j, width : 2 * width]
        coef = packed_ref[j, 2 * width]
        lead_left = jnp.broadcast_to(coef[:, 0:1], (levels, lanes))
        tail_left = jnp.broadcast_to(coef[:, 1:2], (levels, lanes))
        lead_right = jnp.broadcast_to(coef[:, 2:3], (levels, lanes))
        tail_right = jnp.broadcast_to(coef[:, 3:4], (levels, lanes))
        pivot = 1.0 + lead_left * q
        alpha = (first - lead_left * p) / pivot
        beta = -lead_right / pivot
        p_s[j] = p
        q_s[j] = q
        alpha_s[j] = alpha
        beta_s[j] = beta
        p = last - tail_left * p - tail_left * q * alpha
        q = -(tail_left * q * beta) - tail_right
    ahead = jnp.zeros((width, levels, lanes), jnp.float32)
    f_s[count] = ahead
    for j in range(count - 1, -1, -1):
        ahead = alpha_s[j] + beta_s[j] * ahead
        f_s[j] = ahead
    pos = pos_ref[0]
    left = p_s[pos] + q_s[pos] * f_s[pos]
    right = f_s[pos + 1]
    for w in range(width):
        for level in range(levels):
            out_ref[w, level] = (
                solve_ref[w, level]
                - lspike_ref[level] * left[w, level : level + 1, :]
                - rspike_ref[level] * right[w, level : level + 1, :]
            )

def interface_update(packed_all, position, local_solve, left_spike, right_spike):
    count, _, levels, lanes = packed_all.shape
    width = local_solve.shape[0]
    vmem = pltpu.VMEM
    return pl.pallas_call(
        _solve_body,
        out_shape=jax.ShapeDtypeStruct(local_solve.shape, jnp.float32),
        in_specs=[pl.BlockSpec(memory_space=pltpu.SMEM)] + [pl.BlockSpec(memory_space=vmem)] * 4,
        out_specs=pl.BlockSpec(memory_space=vmem),
        scratch_shapes=[
            pltpu.VMEM((count, width, levels, lanes), jnp.float32),
            pltpu.VMEM((count, levels, lanes), jnp.float32),
            pltpu.VMEM((count, width, levels, lanes), jnp.float32),
            pltpu.VMEM((count, levels, lanes), jnp.float32),
            pltpu.VMEM((count + 1, width, levels, lanes), jnp.float32),
        ],
    )(
        jnp.reshape(position, (1,)).astype(jnp.int32),
        packed_all,
        local_solve,
        left_spike[:, :, None],
        right_spike[:, :, None],
    )


def halo_x(block, axis, width):
    count = lax.axis_size(axis)
    forward = [(i, i + 1) for i in range(count - 1)]
    backward = [(target, source) for source, target in forward]
    low = lax.ppermute(block[:, block.shape[1] - width :], axis, forward)
    high = lax.ppermute(block[:, 0:width], axis, backward)
    return jnp.concatenate([low, block, high], axis=1)


def halo_y(block, axis, width):
    count = lax.axis_size(axis)
    forward = [(i, i + 1) for i in range(count - 1)]
    backward = [(target, source) for source, target in forward]
    low = lax.ppermute(block[:, :, block.shape[2] - width :], axis, forward)
    high = lax.ppermute(block[:, :, 0:width], axis, backward)
    return jnp.concatenate([low, high], axis=2)


def source_of(offsets, run, block_count):
    blocks = run * block_count + jnp.arange(block_count, dtype=jnp.int32)
    return blocks - lax.dynamic_slice_in_dim(offsets, run * block_count, block_count)


def slot_rank(mask):
    return jnp.cumsum(mask.astype(jnp.int32)) - 1


def send_windows(main, halo, offsets, position, count, block_count):
    window = BX + 4
    cap = 4
    channels, _, rows_here = main.shape
    deltas = (-2, -1, 1, 2)
    received_main = {}
    received_halo = {}
    for delta in deltas:
        target = jnp.clip(position - delta, 0, count - 1)
        source = source_of(offsets, target, block_count)
        local_start = (source - position * block_count) * BX
        mask = (source >= position * block_count) & (source < (position + 1) * block_count)
        rank = slot_rank(mask)
        starts = [
            jnp.sum(jnp.where(mask & (rank == slot), local_start, 0)) for slot in range(cap)
        ]
        send_main = jnp.concatenate(
            [lax.dynamic_slice_in_dim(main, start, window, 1) for start in starts], axis=1
        )
        send_halo = jnp.concatenate(
            [lax.dynamic_slice_in_dim(halo, start, window, 2) for start in starts], axis=2
        )
        span = cap * window
        send_halo = jnp.pad(send_halo, ((0, 0), (0, 0), (0, rows_here - span)))
        sent = shifted_2(jnp.concatenate([send_main, send_halo], axis=1), "gx", -delta)
        received_main[delta] = sent[:, 0:span]
        received_halo[delta] = sent[:, span:, 0:span]
    return received_main, received_halo


def assemble_windows(main, halo, received_main, received_halo, offsets, position, block_count):
    window = BX + 4
    order = (-2, -1, 0, 1, 2)
    pieces_main = [main if delta == 0 else received_main[delta] for delta in order]
    pieces_halo = [halo if delta == 0 else received_halo[delta] for delta in order]
    bases = {}
    base = 0
    for delta, piece in zip(order, pieces_main):
        bases[delta] = base
        base += piece.shape[1]
    all_main = jnp.concatenate(pieces_main, axis=1)
    all_halo = jnp.concatenate(pieces_halo, axis=2)
    own_source = source_of(offsets, position, block_count)
    own_delta = own_source // block_count - position
    start_here = jnp.zeros((block_count,), jnp.int32)
    for delta in order:
        if delta == 0:
            candidate = bases[0] + (own_source - position * block_count) * BX
        else:
            rank = slot_rank(own_delta == delta)
            candidate = bases[delta] + rank * window
        start_here = jnp.where(own_delta == delta, candidate, start_here)
    window_main = jnp.stack(
        [lax.dynamic_slice_in_dim(all_main, start_here[b], window, 1) for b in range(block_count)]
    )
    window_halo = jnp.stack(
        [lax.dynamic_slice_in_dim(all_halo, start_here[b], window, 2) for b in range(block_count)]
    ).transpose(0, 1, 3, 2)
    return jnp.concatenate(
        [window_halo[..., 0:2], window_main, window_halo[..., 2:4]], axis=3
    )


def advect_group(windows, shift_x, shift_y, field_count):
    block_count = windows.shape[0]
    level_count, columns, rows_here = shift_x.shape
    windows = windows.reshape(block_count, field_count, level_count, BX + 4, rows_here + 4)
    across = shift_x.reshape(level_count, block_count, BX, rows_here).transpose(1, 0, 2, 3)[:, None]
    along = shift_y.reshape(level_count, block_count, BX, rows_here).transpose(1, 0, 2, 3)[:, None]
    interpolated = interpolate(windows, across, along, BX, rows_here)
    return interpolated.transpose(1, 2, 0, 3, 4).reshape(
        field_count, level_count, columns, rows_here
    )


def local(fields, shift_x, shift_y, block_offset, group_inverse, lower_coupling, upper_coupling):
    field_count, level_count, columns, rows_here = fields.shape
    block_count = columns // BX
    channels = field_count * level_count
    wind_channels = 2 * level_count
    count = lax.axis_size("gx")
    position = lax.axis_index("gx")
    flat = fields.reshape(channels, columns, rows_here)
    main = halo_x(flat, "gx", 2)
    halo = halo_y(main, "gy", 2).transpose(0, 2, 1)
    offsets = block_offset[:, 0]
    wind_main, wind_halo = main[:wind_channels], halo[:wind_channels]
    tracer_main, tracer_halo = main[wind_channels:], halo[wind_channels:]
    wind_received = send_windows(wind_main, wind_halo, offsets, position, count, block_count)
    tracer_received = send_windows(tracer_main, tracer_halo, offsets, position, count, block_count)
    wind_windows = assemble_windows(
        wind_main, wind_halo, *wind_received, offsets, position, block_count
    )
    winds = advect_group(wind_windows, shift_x, shift_y, 2)
    local_solve = jnp.einsum("lij,wljy->wliy", group_inverse, winds, precision=PRECISE)
    lower_here = lower_coupling[:, 0]
    upper_here = upper_coupling[:, 0]
    left_spike = group_inverse[:, :, 0] * lower_here[:, None]
    right_spike = group_inverse[:, :, columns - 1] * upper_here[:, None]
    coef = jnp.stack(
        [left_spike[:, 0], left_spike[:, columns - 1], right_spike[:, 0], right_spike[:, columns - 1]],
        axis=-1,
    )
    coef_rows = jnp.pad(coef, ((0, 0), (0, rows_here - 4)))
    first_row = local_solve[:, :, 0, :]
    last_row = local_solve[:, :, columns - 1, :]
    packed = jnp.concatenate([first_row, last_row, coef_rows[None]], axis=0)
    held = packed[None]
    step = 1
    while step < count:
        ring = [(i, (i + step) % count) for i in range(count)]
        held = jnp.concatenate([held, lax.ppermute(held, "gx", ring)], axis=0)
        if step == 1:
            held, tracer_received = lax.optimization_barrier((held, tracer_received))
        step *= 2
    reverse = held[::-1]
    doubled = jnp.concatenate([reverse, reverse], axis=0)
    packed_all = lax.dynamic_slice_in_dim(doubled, count - 1 - position, count, 0)
    wind_fields = interface_update(packed_all, position, local_solve, left_spike, right_spike)
    tracer_windows = assemble_windows(
        tracer_main, tracer_halo, *tracer_received, offsets, position, block_count
    )
    tracers = advect_group(tracer_windows, shift_x, shift_y, field_count - 2)
    return (wind_fields, tracers)


def solution(mesh):
    return jax.shard_map(
        local,
        mesh=mesh,
        in_specs=(
            P(None, None, "gx", "gy"),
            P(None, "gx", "gy"),
            P(None, "gx", "gy"),
            P(None, "gy"),
            P(None, "gx", None),
            P(None, "gx"),
            P(None, "gx"),
        ),
        out_specs=(P(None, None, "gx", "gy"), P(None, None, "gx", "gy")),
        check_vma=False,
    )
```

```python
import jax
import jax.numpy as jnp
from jax import lax
from jax.sharding import PartitionSpec as P
from jax.experimental import pallas as pl
from jax.experimental.pallas import tpu as pltpu

BX = 16


PRECISE = lax.Precision.HIGHEST


def padded_2(block, sides, width):
    for axis, dim in sides:
        count = lax.axis_size(axis)
        forward = [(i, i + 1) for i in range(count - 1)]
        backward = [(target, source) for source, target in forward]
        low = lax.ppermute(
            lax.slice_in_dim(block, block.shape[dim] - width, None, axis=dim), axis, forward
        )
        high = lax.ppermute(lax.slice_in_dim(block, 0, width, axis=dim), axis, backward)
        block = jnp.concatenate([low, block, high], axis=dim)
    return block


def shifted_2(value, axis, steps):
    count = lax.axis_size(axis)
    leading, last = (max(0, -steps), min(count, count - steps))
    return lax.ppermute(value, axis, [(source, source + steps) for source in range(leading, last)])


def lagrange(displace):
    position = -displace
    weights = []
    for target in range(-2, 3):
        factor = jnp.ones_like(position)
        for anchor in range(-2, 3):
            if anchor != target:
                factor = factor * ((position - anchor) / (target - anchor))
        weights.append(factor)
    return weights


def interpolate(window, across, along, span_x, span_y):
    weights_x = lagrange(across)
    weights_y = lagrange(along)
    running_total = None
    for column_tap in range(5):
        partial_sum = weights_y[0] * window[..., column_tap : column_tap + span_x, 0:span_y]
        for row_tap in range(1, 5):
            partial_sum = (
                partial_sum
                + weights_y[row_tap]
                * window[..., column_tap : column_tap + span_x, row_tap : row_tap + span_y]
            )
        tap_term = weights_x[column_tap] * partial_sum
        running_total = tap_term if running_total is None else running_total + tap_term
    return running_total


def _solve_body(pos_ref, packed_ref, solve_ref, lspike_ref, rspike_ref, out_ref, alpha_s, beta_s, p_s, q_s, f_s):
    count = packed_ref.shape[0]
    width, levels = out_ref.shape[0], out_ref.shape[1]
    lanes = out_ref.shape[3]
    p = jnp.zeros((width, levels, lanes), jnp.float32)
    q = jnp.zeros((levels, lanes), jnp.float32)
    pos = pos_ref[0]
    for j in range(count):
        held_at = (pos - j + count) % count
        first = packed_ref[held_at, 0:width]
        last = packed_ref[held_at, width : 2 * width]
        coef = packed_ref[held_at, 2 * width]
        lead_left = jnp.broadcast_to(coef[:, 0:1], (levels, lanes))
        tail_left = jnp.broadcast_to(coef[:, 1:2], (levels, lanes))
        lead_right = jnp.broadcast_to(coef[:, 2:3], (levels, lanes))
        tail_right = jnp.broadcast_to(coef[:, 3:4], (levels, lanes))
        pivot = 1.0 + lead_left * q
        alpha = (first - lead_left * p) / pivot
        beta = -lead_right / pivot
        p_s[j] = p
        q_s[j] = q
        alpha_s[j] = alpha
        beta_s[j] = beta
        p = last - tail_left * p - tail_left * q * alpha
        q = -(tail_left * q * beta) - tail_right
    ahead = jnp.zeros((width, levels, lanes), jnp.float32)
    f_s[count] = ahead
    for j in range(count - 1, -1, -1):
        ahead = alpha_s[j] + beta_s[j] * ahead
        f_s[j] = ahead
    left = p_s[pos] + q_s[pos] * f_s[pos]
    right = f_s[pos + 1]
    for w in range(width):
        for level in range(levels):
            out_ref[w, level] = (
                solve_ref[w, level]
                - lspike_ref[level] * left[w, level : level + 1, :]
                - rspike_ref[level] * right[w, level : level + 1, :]
            )

def interface_update(packed_all, position, local_solve, left_spike, right_spike):
    count, _, levels, lanes = packed_all.shape
    width = local_solve.shape[0]
    vmem = pltpu.VMEM
    return pl.pallas_call(
        _solve_body,
        out_shape=jax.ShapeDtypeStruct(local_solve.shape, jnp.float32),
        in_specs=[pl.BlockSpec(memory_space=pltpu.SMEM)] + [pl.BlockSpec(memory_space=vmem)] * 4,
        out_specs=pl.BlockSpec(memory_space=vmem),
        scratch_shapes=[
            pltpu.VMEM((count, width, levels, lanes), jnp.float32),
            pltpu.VMEM((count, levels, lanes), jnp.float32),
            pltpu.VMEM((count, width, levels, lanes), jnp.float32),
            pltpu.VMEM((count, levels, lanes), jnp.float32),
            pltpu.VMEM((count + 1, width, levels, lanes), jnp.float32),
        ],
    )(
        jnp.reshape(position, (1,)).astype(jnp.int32),
        packed_all,
        local_solve,
        left_spike[:, :, None],
        right_spike[:, :, None],
    )


def halo_x(block, axis, width):
    count = lax.axis_size(axis)
    forward = [(i, i + 1) for i in range(count - 1)]
    backward = [(target, source) for source, target in forward]
    low = lax.ppermute(block[:, block.shape[1] - width :], axis, forward)
    high = lax.ppermute(block[:, 0:width], axis, backward)
    return jnp.concatenate([low, block, high], axis=1)


def halo_y(block, axis, width):
    count = lax.axis_size(axis)
    forward = [(i, i + 1) for i in range(count - 1)]
    backward = [(target, source) for source, target in forward]
    low = lax.ppermute(block[:, :, block.shape[2] - width :], axis, forward)
    high = lax.ppermute(block[:, :, 0:width], axis, backward)
    return jnp.concatenate([low, high], axis=2)


def source_of(offsets, run, block_count):
    blocks = run * block_count + jnp.arange(block_count, dtype=jnp.int32)
    return blocks - lax.dynamic_slice_in_dim(offsets, run * block_count, block_count)


def slot_rank(mask):
    return jnp.cumsum(mask.astype(jnp.int32)) - 1


def send_windows(main, halo, offsets, position, count, block_count):
    window = BX + 4
    cap = 4
    channels, _, rows_here = main.shape
    deltas = (-2, -1, 1, 2)
    received_main = {}
    received_halo = {}
    for delta in deltas:
        target = jnp.clip(position - delta, 0, count - 1)
        source = source_of(offsets, target, block_count)
        local_start = (source - position * block_count) * BX
        mask = (source >= position * block_count) & (source < (position + 1) * block_count)
        rank = slot_rank(mask)
        starts = [
            jnp.sum(jnp.where(mask & (rank == slot), local_start, 0)) for slot in range(cap)
        ]
        send_main = jnp.concatenate(
            [lax.dynamic_slice_in_dim(main, start, window, 1) for start in starts], axis=1
        )
        send_halo = jnp.concatenate(
            [lax.dynamic_slice_in_dim(halo, start, window, 2) for start in starts], axis=2
        )
        span = cap * window
        send_halo = jnp.pad(send_halo, ((0, 0), (0, 0), (0, rows_here - span)))
        sent = shifted_2(jnp.concatenate([send_main, send_halo], axis=1), "gx", -delta)
        received_main[delta] = sent[:, 0:span]
        received_halo[delta] = sent[:, span:, 0:span]
    return received_main, received_halo


def assemble_windows(main, halo, received_main, received_halo, offsets, position, block_count):
    window = BX + 4
    order = (-2, -1, 0, 1, 2)
    pieces_main = [main if delta == 0 else received_main[delta] for delta in order]
    pieces_halo = [halo if delta == 0 else received_halo[delta] for delta in order]
    bases = {}
    base = 0
    for delta, piece in zip(order, pieces_main):
        bases[delta] = base
        base += piece.shape[1]
    all_main = jnp.concatenate(pieces_main, axis=1)
    all_halo = jnp.concatenate(pieces_halo, axis=2)
    own_source = source_of(offsets, position, block_count)
    own_delta = own_source // block_count - position
    start_here = jnp.zeros((block_count,), jnp.int32)
    for delta in order:
        if delta == 0:
            candidate = bases[0] + (own_source - position * block_count) * BX
        else:
            rank = slot_rank(own_delta == delta)
            candidate = bases[delta] + rank * window
        start_here = jnp.where(own_delta == delta, candidate, start_here)
    window_main = jnp.stack(
        [lax.dynamic_slice_in_dim(all_main, start_here[b], window, 1) for b in range(block_count)]
    )
    window_halo = jnp.stack(
        [lax.dynamic_slice_in_dim(all_halo, start_here[b], window, 2) for b in range(block_count)]
    ).transpose(0, 1, 3, 2)
    return jnp.concatenate(
        [window_halo[..., 0:2], window_main, window_halo[..., 2:4]], axis=3
    )


def advect_group(windows, shift_x, shift_y, field_count):
    block_count = windows.shape[0]
    level_count, columns, rows_here = shift_x.shape
    windows = windows.reshape(block_count, field_count, level_count, BX + 4, rows_here + 4)
    across = shift_x.reshape(level_count, block_count, BX, rows_here).transpose(1, 0, 2, 3)[:, None]
    along = shift_y.reshape(level_count, block_count, BX, rows_here).transpose(1, 0, 2, 3)[:, None]
    interpolated = interpolate(windows, across, along, BX, rows_here)
    return interpolated.transpose(1, 2, 0, 3, 4).reshape(
        field_count, level_count, columns, rows_here
    )


def local(fields, shift_x, shift_y, block_offset, group_inverse, lower_coupling, upper_coupling):
    field_count, level_count, columns, rows_here = fields.shape
    block_count = columns // BX
    channels = field_count * level_count
    wind_channels = 2 * level_count
    count = lax.axis_size("gx")
    position = lax.axis_index("gx")
    flat = fields.reshape(channels, columns, rows_here)
    main = halo_x(flat, "gx", 2)
    halo = halo_y(main, "gy", 2).transpose(0, 2, 1)
    offsets = block_offset[:, 0]
    wind_main, wind_halo = main[:wind_channels], halo[:wind_channels]
    tracer_main, tracer_halo = main[wind_channels:], halo[wind_channels:]
    wind_received = send_windows(wind_main, wind_halo, offsets, position, count, block_count)
    tracer_received = send_windows(tracer_main, tracer_halo, offsets, position, count, block_count)
    wind_windows = assemble_windows(
        wind_main, wind_halo, *wind_received, offsets, position, block_count
    )
    winds = advect_group(wind_windows, shift_x, shift_y, 2)
    local_solve = jnp.einsum("lij,wljy->wliy", group_inverse, winds, precision=PRECISE)
    lower_here = lower_coupling[:, 0]
    upper_here = upper_coupling[:, 0]
    left_spike = group_inverse[:, :, 0] * lower_here[:, None]
    right_spike = group_inverse[:, :, columns - 1] * upper_here[:, None]
    coef = jnp.stack(
        [left_spike[:, 0], left_spike[:, columns - 1], right_spike[:, 0], right_spike[:, columns - 1]],
        axis=-1,
    )
    coef_rows = jnp.pad(coef, ((0, 0), (0, rows_here - 4)))
    first_row = local_solve[:, :, 0, :]
    last_row = local_solve[:, :, columns - 1, :]
    packed = jnp.concatenate([first_row, last_row, coef_rows[None]], axis=0)
    held = packed[None]
    step = 1
    while step < count:
        ring = [(i, (i + step) % count) for i in range(count)]
        held = jnp.concatenate([held, lax.ppermute(held, "gx", ring)], axis=0)
        if step == 1:
            held, tracer_received = lax.optimization_barrier((held, tracer_received))
        step *= 2
    packed_all = held
    wind_fields = interface_update(packed_all, position, local_solve, left_spike, right_spike)
    tracer_windows = assemble_windows(
        tracer_main, tracer_halo, *tracer_received, offsets, position, block_count
    )
    tracers = advect_group(tracer_windows, shift_x, shift_y, field_count - 2)
    return (wind_fields, tracers)


def solution(mesh):
    return jax.shard_map(
        local,
        mesh=mesh,
        in_specs=(
            P(None, None, "gx", "gy"),
            P(None, "gx", "gy"),
            P(None, "gx", "gy"),
            P(None, "gy"),
            P(None, "gx", None),
            P(None, "gx"),
            P(None, "gx"),
        ),
        out_specs=(P(None, None, "gx", "gy"), P(None, None, "gx", "gy")),
        check_vma=False,
    )
```
